32 devices in a mesh: pipe: 4 (over z), sx: 4 (over y, x), sy: 2 (over core).
Axes of the slice: x: 2, y: 2, z: 4, core: 2. Of those that a mesh axis runs over, the one named last changes fastest.
Arguments:
- segment_inputs: bfloat16 [4, 1, 4, 2, 512, 128], P('pipe', None, 'sx', 'sy'), may hold values from -6 to 6
- out_cotangent: bfloat16 [1, 4, 2, 512, 128], P(None, 'sx', 'sy'), may hold values from -6 to 6
- neighbours: int32 [1, 4, 2, 1, 27], P(None, 'sx', 'sy'), may hold values from 0 to 1, as said below
- block_counts: int32 [1, 4, 2], P(None, 'sx', 'sy'), may hold values from 1 to 1, as said below
- norm_gain: float32 [4, 128], P('pipe'), may hold values from 0.1 to 1.9
- kernel: bfloat16 [4, 3456, 128], P('pipe', 'sx'), may hold values from -0.109375 to 0.109375
Outputs:
- grad_inputs: bfloat16 [4, 1, 4, 2, 512, 128], P('pipe', None, 'sx', 'sy')
- kernel_grad: float32 [4, 3456, 128], P('pipe', 'sx')
The draws below stay inside these ranges and needn't reach their ends.
Inputs may be any that keep to these rules, and one draw needn't show every extreme that they name: `neighbours`: entry [m, a, b, s, (i + 1) * 9 + (j + 1) * 3 + (k + 1)], i, j, k in -1..1, is the slot in the list of slab (a + i, b + j) of the occupied block lying i, j, k blocks from slot s of slab (a, b) along x, y, z, or 1 where that block is not occupied, the slab is off the grid, or slot s is padding; it never names a padding slot. `block_counts`: slots 0 to count - 1 of a slab's list hold its occupied blocks; later slots are padding.
All inputs are finite; a program needn't handle non-finite values.
Results may differ from the reference program's by a relative error of at most 0.014.
Values may be sent and summed in bfloat16 or wider, within the bound.
No kernel may reach another device: no remote copies, remote signals or barrier semaphores. Data moves between devices by JAX's collectives and lax.ppermute only.
A program may use at most 64 MiB of HBM per device.

```python
import jax
import jax.numpy as jnp
from jax import lax

C = 128
NB = 1
MB = 1
SEGMENTS = 4
VOXELS = 4096
N_SX = 4
N_SY = 2


def block_geometry(key):
    base_key = jax.random.fold_in(key, 11)
    key_x, key_y, key_count = jax.random.split(base_key, 3)
    steps_x = jax.random.randint(key_x, (MB, N_SX), -1, 2)
    steps_y = jax.random.randint(key_y, (MB, N_SY), -1, 2)
    height = jnp.cumsum(steps_x, axis=1)[:, :, None] + jnp.cumsum(steps_y, axis=1)[:, None, :]
    counts = jax.random.randint(key_count, (MB, N_SX, N_SY), 1, NB + 1)
    counts = counts.at[:, 0, 0].set(NB)
    return (height.astype(jnp.int32), counts.astype(jnp.int32))


def draw_block_counts(key, part):
    return block_geometry(key)[1]


def draw_neighbours(key, part):
    height, counts = block_geometry(key)
    slot_ids = jnp.arange(NB, dtype=jnp.int32)
    padded_height = jnp.pad(height, ((0, 0), (1, 1), (1, 1)))
    padded_counts = jnp.pad(counts, ((0, 0), (1, 1), (1, 1)))
    entries = []
    for shift_x in (-1, 0, 1):
        for shift_y in (-1, 0, 1):
            other_height = padded_height[:, 1 + shift_x:1 + shift_x + N_SX, 1 + shift_y:1 + shift_y + N_SY]
            other_counts = padded_counts[:, 1 + shift_x:1 + shift_x + N_SX, 1 + shift_y:1 + shift_y + N_SY]
            for shift_z in (-1, 0, 1):
                target = height[..., None] + slot_ids + shift_z - other_height[..., None]
                usable = (target >= 0) & (target < other_counts[..., None]) & (slot_ids < counts[..., None])
                entries.append(jnp.where(usable, target, NB))
    return jnp.stack(entries, axis=-1).astype(jnp.int32)


def steps_of(rng, shape, cuts, least, high):
    gain, own = 1.0, jax.random.fold_in(rng, 6)
    for axis_at, shards_of in cuts:
        heights = jnp.exp(jax.random.uniform(jax.random.fold_in(own, axis_at), (shards_of,), jnp.float32, least / len(cuts), high / len(cuts)))
        gain = gain * jnp.repeat(heights, shape[axis_at] // shards_of).reshape([-1 if axis == axis_at else 1 for axis in range(len(shape))])
    return gain


def centred(rng, dims, width, most, cuts=(), kind=jnp.bfloat16):
    gain = steps_of(rng, dims, cuts, -0.22, 0.18) if cuts else 1.0
    values = jax.random.normal(rng, dims, jnp.float32) * width * gain
    return jnp.minimum(jnp.maximum(values, -most), most).astype(kind)


def setup_inputs(seed: int = 0) -> dict:
    key_list = jax.random.split(jax.random.key(seed), 7)
    return {
        "segment_inputs": centred(key_list[0], (SEGMENTS, MB, N_SX, N_SY, NB * 512, C), 1.0, 6.0, ((0, 4), (2, 4), (3, 2))),
        "out_cotangent": centred(key_list[1], (MB, N_SX, N_SY, NB * 512, C), 1.0, 6.0, ((1, 4), (2, 2))),
        "neighbours": draw_neighbours(jax.random.fold_in(key_list[6], 71), 0),
        "block_counts": draw_block_counts(jax.random.fold_in(key_list[6], 71), 0),
        "norm_gain": jnp.clip(1.0 + 0.18 * jax.random.normal(key_list[4], (SEGMENTS, C), jnp.float32), 0.1, 1.9),
        "kernel": centred(key_list[5], (SEGMENTS, 27 * C, C), (27 * C) ** -0.5, 0.109375, ((0, 4), (1, 4))),
    }


OFFSETS = (-1, 0, 1)

def source_range(offset):
    if offset < 0:
        return slice(7, 8)
    if offset > 0:
        return slice(0, 1)
    return slice(0, 8)

def activate(values, gain_row):
    floats = values.astype(jnp.float32)
    square = lax.optimization_barrier(jnp.mean(floats * floats, axis=-1, keepdims=True))
    return jax.nn.silu(floats * lax.rsqrt(square + 1e-06) * gain_row)

def assemble(sources, table):
    slabs_x = []
    for shift_x in OFFSETS:
        rows_y = []
        for shift_y in OFFSETS:
            column = (shift_x + 1) * 3 + (shift_y + 1)
            parts_z = []
            for shift_z in OFFSETS:
                direction = column * 3 + shift_z + 1
                picked = sources[column][table[:, direction]]
                parts_z.append(picked[:, :, :, source_range(shift_z), :])
            rows_y.append(jnp.concatenate(parts_z, axis=3))
        slabs_x.append(jnp.concatenate(rows_y, axis=2))
    return jnp.concatenate(slabs_x, axis=1)

def backward_local(values, grad_live, live_now, act_pad, grad_pad, weights, gain_row):
    row_count, channels = values.shape
    grad_act = jnp.zeros((row_count, channels), jnp.float32)
    pieces = []
    for tap_x in OFFSETS:
        for tap_y in OFFSETS:
            for tap_z in OFFSETS:
                tap_index = (tap_x + 1) * 9 + (tap_y + 1) * 3 + (tap_z + 1)
                weight = weights[tap_index * channels:(tap_index + 1) * channels]
                shifted_act = act_pad[:, 1 + tap_x:9 + tap_x, 1 + tap_y:9 + tap_y, 1 + tap_z:9 + tap_z, :].reshape(row_count, channels)
                shifted_grad = grad_pad[:, 1 - tap_x:9 - tap_x, 1 - tap_y:9 - tap_y, 1 - tap_z:9 - tap_z, :].reshape(row_count, channels)
                pieces.append(jnp.dot(shifted_act.T, grad_live, preferred_element_type=jnp.float32))
                grad_act = grad_act + jnp.dot(shifted_grad, weight.T, preferred_element_type=jnp.float32)
    _, pullback = jax.vjp(lambda floats: activate(floats, gain_row), values.astype(jnp.float32))
    through, = pullback(grad_act)
    summed = grad_live.astype(jnp.float32) + through
    result = jnp.where(live_now[:, None], summed, jnp.zeros_like(summed))
    return (result.astype(jnp.bfloat16), jnp.concatenate(pieces, axis=0))

def neighbour_sources(field, blocks):
    cube_view = field.reshape(field.shape[0], field.shape[1], blocks, 8, 8, 8, field.shape[-1])
    padded = jnp.pad(cube_view, ((1, 1), (1, 1), (0, 0), (0, 0), (0, 0), (0, 0), (0, 0)))
    sources = []
    for shift_x in OFFSETS:
        for shift_y in OFFSETS:
            moved_cubes = padded[1 + shift_x:1 + shift_x + cube_view.shape[0], 1 + shift_y:1 + shift_y + cube_view.shape[1]]
            moved_cubes = moved_cubes[:, :, :, source_range(shift_x), source_range(shift_y)]
            blank_cube = jnp.zeros_like(moved_cubes[:, :, :1])
            sources.append(jnp.concatenate([moved_cubes, blank_cube], axis=2))
    return sources

def device_step(act_sources, grad_sources, table, values, grad_live, live_now, weights, gain_row):
    act_pad = assemble(act_sources, table)
    grad_pad = assemble(grad_sources, table)
    return backward_local(values, grad_live, live_now, act_pad, grad_pad, weights, gain_row)

def reference(segment_inputs, out_cotangent, neighbours, block_counts, norm_gain, kernel):
    segment_count = segment_inputs.shape[0]
    micro_count = segment_inputs.shape[1]
    row_count = segment_inputs.shape[4]
    blocks = row_count // 512
    slot_ids = jnp.arange(row_count, dtype=jnp.int32) // 512
    live_rows = slot_ids[None, None, None, :] < block_counts[..., None]
    axes_map = (0, 0, 0, 0, 0, 0, None, None)
    per_device = jax.vmap(jax.vmap(device_step, in_axes=axes_map), in_axes=axes_map)
    upstream = []
    for micro_index in range(micro_count):
        cotangent = out_cotangent[micro_index]
        upstream.append(jnp.where(live_rows[micro_index][..., None], cotangent, jnp.zeros_like(cotangent)))
    grad_list = []
    kernel_list = []
    for segment_index in reversed(range(segment_count)):
        kernel_total = jnp.zeros(kernel.shape[1:], jnp.float32)
        results = []
        for micro_index in range(micro_count):
            values = segment_inputs[segment_index, micro_index]
            activation = activate(values, norm_gain[segment_index]).astype(jnp.bfloat16)
            result, pieces = per_device(neighbour_sources(activation, blocks), neighbour_sources(upstream[micro_index], blocks), neighbours[micro_index], values, upstream[micro_index], live_rows[micro_index], kernel[segment_index], norm_gain[segment_index])
            results.append(result)
            kernel_total = kernel_total + lax.optimization_barrier(jnp.sum(pieces, axis=(0, 1)))
        upstream = results
        grad_list.insert(0, jnp.stack(results))
        kernel_list.insert(0, kernel_total / jnp.sqrt(jnp.float32(VOXELS)))
    return (jnp.stack(grad_list), jnp.stack(kernel_list))
```

```python
import jax
import jax.numpy as jnp
from jax import lax
from jax.sharding import PartitionSpec as P

OFFSETS = (-1, 0, 1)


def source_range(offset):
    if offset < 0:
        return slice(7, 8)
    if offset > 0:
        return slice(0, 1)
    return slice(0, 8)


def activate(values, gain_row):
    floats = values.astype(jnp.float32)
    square = jnp.mean(floats * floats, axis=-1, keepdims=True)
    return jax.nn.silu(floats * lax.rsqrt(square + 1e-06) * gain_row)


def with_blank(blocks_in):
    return jnp.concatenate([blocks_in, jnp.zeros_like(blocks_in)], axis=0)


def face_piece(cube, shift_x, shift_y):
    return cube[:, source_range(shift_x), source_range(shift_y)]


def directions():
    return [(sx, sy) for sx in OFFSETS for sy in OFFSETS if (sx, sy) != (0, 0)]


def assemble(centre, received, table):
    slabs_x = []
    for shift_x in OFFSETS:
        rows_y = []
        for shift_y in OFFSETS:
            column = (shift_x + 1) * 3 + (shift_y + 1)
            source = with_blank(centre if (shift_x, shift_y) == (0, 0) else received[(shift_x, shift_y)])
            parts_z = []
            for shift_z in OFFSETS:
                direction = column * 3 + shift_z + 1
                picked = source[table[:, direction]]
                parts_z.append(picked[:, :, :, source_range(shift_z), :])
            rows_y.append(jnp.concatenate(parts_z, axis=3))
        slabs_x.append(jnp.concatenate(rows_y, axis=2))
    return jnp.concatenate(slabs_x, axis=1)


def exchange(cube, axes, sizes, pipe_step):
    received = {}
    for shift_x, shift_y in directions():
        piece = face_piece(cube, shift_x, shift_y)
        route = []
        if pipe_step:
            n_pipe, n_x, n_y = sizes
            for p in range(pipe_step, n_pipe):
                for a in range(n_x):
                    for b in range(n_y):
                        ta, tb = a - shift_x, b - shift_y
                        if 0 <= ta < n_x and 0 <= tb < n_y:
                            route.append(((p * n_x + a) * n_y + b, ((p - pipe_step) * n_x + ta) * n_y + tb))
        else:
            n_x, n_y = sizes
            for a in range(n_x):
                for b in range(n_y):
                    ta, tb = a - shift_x, b - shift_y
                    if 0 <= ta < n_x and 0 <= tb < n_y:
                        route.append((a * n_y + b, ta * n_y + tb))
        received[(shift_x, shift_y)] = lax.ppermute(piece, axes, route)
    return received


def columns(padded, rows, sign):
    taps = []
    for tap_x in OFFSETS:
        for tap_y in OFFSETS:
            for tap_z in OFFSETS:
                taps.append(
                    padded[
                        :,
                        1 + sign * tap_x : 9 + sign * tap_x,
                        1 + sign * tap_y : 9 + sign * tap_y,
                        1 + sign * tap_z : 9 + sign * tap_z,
                        :,
                    ]
                )
    stacked = jnp.stack(taps, axis=-2)
    return stacked.reshape(rows, len(taps) * padded.shape[-1])


def finish_grad(values, grad_live, live_now, grad_act, gain_row):
    _, pullback = jax.vjp(lambda floats: activate(floats, gain_row), values.astype(jnp.float32))
    (through,) = pullback(grad_act)
    summed = grad_live.astype(jnp.float32) + through
    result = jnp.where(live_now[:, None], summed, jnp.zeros_like(summed))
    return result.astype(jnp.bfloat16)


def shards(segment_inputs, out_cotangent, neighbours, block_counts, norm_gain, kernel):
    n_pipe = lax.axis_size("pipe")
    n_x = lax.axis_size("sx")
    n_y = lax.axis_size("sy")
    segment_place = lax.axis_index("pipe")
    micro_count = segment_inputs.shape[1]
    row_count = segment_inputs.shape[4]
    channels = segment_inputs.shape[5]
    blocks = row_count // 512
    taps = 27
    weights = lax.all_gather(kernel[0], "sx", axis=0, tiled=True)
    flipped = weights.reshape(taps, channels, channels).transpose(0, 2, 1).reshape(taps * channels, channels)
    gain_row = norm_gain[0]
    inputs = segment_inputs[0, :, 0, 0]
    cotangent = out_cotangent[:, 0, 0]
    tables = neighbours[:, 0, 0]
    slot_ids = jnp.arange(row_count, dtype=jnp.int32) // 512
    live_rows = slot_ids[None, :] < block_counts[:, 0, 0][:, None]

    def cube(values):
        return values.reshape(blocks, 8, 8, 8, channels)

    grads_out = []
    kernel_total = jnp.zeros((taps * channels, channels), jnp.float32)
    for micro in range(micro_count):
        table = tables[micro]
        live_now = live_rows[micro]
        values = inputs[micro]
        activation = activate(values, gain_row).astype(jnp.bfloat16)
        start = cotangent[micro]
        start = jnp.where(live_now[:, None], start, jnp.zeros_like(start))
        both = jnp.concatenate([cube(activation), cube(start)], axis=-1)
        got = exchange(both, ("sx", "sy"), (n_x, n_y), 0)
        act_pad = assemble(cube(activation), {k: v[..., :channels] for k, v in got.items()}, table)
        act_cols = columns(act_pad, row_count, 1)
        centre = start
        received = {k: v[..., channels:] for k, v in got.items()}
        kept_dy = start
        kept_grad = jnp.zeros((row_count, channels), jnp.bfloat16)
        for tick in range(n_pipe):
            active = segment_place == n_pipe - 1 - tick
            grad_pad = assemble(cube(centre), received, table)
            grad_act = jnp.dot(columns(grad_pad, row_count, -1), flipped, preferred_element_type=jnp.float32)
            result = finish_grad(values, centre, live_now, grad_act, gain_row)
            kept_dy = jnp.where(active, centre, kept_dy)
            kept_grad = jnp.where(active, result, kept_grad)
            if tick < n_pipe - 1:
                down = [(p, p - 1) for p in range(1, n_pipe)]
                centre = lax.ppermute(result, "pipe", down)
                received = exchange(cube(result), ("pipe", "sx", "sy"), (n_pipe, n_x, n_y), 1)
        kernel_total = kernel_total + lax.dot_general(
            act_cols, kept_dy, (((0,), (0,)), ((), ())), preferred_element_type=jnp.float32
        )
        grads_out.append(kept_grad)
    grad_store = jnp.stack(grads_out)
    norm_scale = float(n_x * n_y * micro_count * row_count) ** (-0.5)
    kernel_term = kernel_total * norm_scale
    shard_rows = kernel.shape[1]
    summed = lax.psum(kernel_term.astype(jnp.bfloat16), "sy").astype(jnp.float32)
    kernel_share = lax.psum_scatter(
        lax.slice_in_dim(summed, 0, shard_rows * n_x, axis=0).astype(jnp.bfloat16),
        "sx",
        scatter_dimension=0,
        tiled=True,
    ).astype(jnp.float32)
    return (grad_store[None, :, None, None], kernel_share[None])


def solution(mesh):
    return jax.shard_map(
        shards,
        mesh=mesh,
        in_specs=(
            P("pipe", None, "sx", "sy", None, None),
            P(None, "sx", "sy", None, None),
            P(None, "sx", "sy", None, None),
            P(None, "sx", "sy"),
            P("pipe", None),
            P("pipe", "sx", None),
        ),
        out_specs=(P("pipe", None, "sx", "sy", None, None), P("pipe", "sx", None)),
        check_vma=False,
    )
```

```python
import jax
import jax.numpy as jnp
from jax import lax
from jax.sharding import PartitionSpec as P

OFFSETS = (-1, 0, 1)


def source_range(offset):
    if offset < 0:
        return slice(7, 8)
    if offset > 0:
        return slice(0, 1)
    return slice(0, 8)


def activate(values, gain_row):
    floats = values.astype(jnp.float32)
    square = jnp.mean(floats * floats, axis=-1, keepdims=True)
    return jax.nn.silu(floats * lax.rsqrt(square + 1e-06) * gain_row)


def with_blank(blocks_in):
    return jnp.concatenate([blocks_in, jnp.zeros_like(blocks_in)], axis=0)


def face_piece(cube, shift_x, shift_y):
    return cube[:, source_range(shift_x), source_range(shift_y)]


def directions():
    return [(sx, sy) for sx in OFFSETS for sy in OFFSETS if (sx, sy) != (0, 0)]


def assemble(centre, received, table):
    slabs_x = []
    for shift_x in OFFSETS:
        rows_y = []
        for shift_y in OFFSETS:
            column = (shift_x + 1) * 3 + (shift_y + 1)
            source = with_blank(centre if (shift_x, shift_y) == (0, 0) else received[(shift_x, shift_y)])
            parts_z = []
            for shift_z in OFFSETS:
                direction = column * 3 + shift_z + 1
                picked = source[table[:, direction]]
                parts_z.append(picked[:, :, :, source_range(shift_z), :])
            rows_y.append(jnp.concatenate(parts_z, axis=3))
        slabs_x.append(jnp.concatenate(rows_y, axis=2))
    return jnp.concatenate(slabs_x, axis=1)


def exchange(cube, axes, sizes, pipe_step):
    received = {}
    for shift_x, shift_y in directions():
        piece = face_piece(cube, shift_x, shift_y)
        route = []
        if pipe_step:
            n_pipe, n_x, n_y = sizes
            for p in range(pipe_step, n_pipe):
                for a in range(n_x):
                    for b in range(n_y):
                        ta, tb = a - shift_x, b - shift_y
                        if 0 <= ta < n_x and 0 <= tb < n_y:
                            route.append(((p * n_x + a) * n_y + b, ((p - pipe_step) * n_x + ta) * n_y + tb))
        else:
            n_x, n_y = sizes
            for a in range(n_x):
                for b in range(n_y):
                    ta, tb = a - shift_x, b - shift_y
                    if 0 <= ta < n_x and 0 <= tb < n_y:
                        route.append((a * n_y + b, ta * n_y + tb))
        received[(shift_x, shift_y)] = lax.ppermute(piece, axes, route)
    return received


def conv_data(padded, filters):
    return lax.conv_general_dilated(
        padded,
        filters,
        (1, 1, 1),
        "VALID",
        dimension_numbers=("NDHWC", "DHWIO", "NDHWC"),
        preferred_element_type=jnp.float32,
    )


def conv_filter(padded, grad_cube):
    return lax.conv_general_dilated(
        padded,
        grad_cube,
        (1, 1, 1),
        "VALID",
        dimension_numbers=("CDHWN", "IDHWO", "NDHWC"),
        preferred_element_type=jnp.float32,
    )


def gathered(shard, axis):
    count = lax.axis_size(axis)
    place = lax.axis_index(axis)
    parts = [shard]
    for step in range(1, count):
        parts.append(lax.ppermute(shard, axis, [(i, (i + step) % count) for i in range(count)]))
    ordered = jnp.stack(parts)
    index = (place - jnp.arange(count)) % count
    slots = jnp.zeros((count,), jnp.int32).at[index].set(jnp.arange(count, dtype=jnp.int32))
    return ordered[slots].reshape(count * shard.shape[0], *shard.shape[1:])


def scattered_sum(full, axis, share_rows):
    count = lax.axis_size(axis)
    place = lax.axis_index(axis)
    total = lax.dynamic_slice_in_dim(full, place * share_rows, share_rows, axis=0).astype(jnp.float32)
    for step in range(1, count):
        target = (place + step) % count
        piece = lax.dynamic_slice_in_dim(full, target * share_rows, share_rows, axis=0)
        total = total + lax.ppermute(piece, axis, [(i, (i + step) % count) for i in range(count)]).astype(
            jnp.float32
        )
    return total


def finish_grad(values, grad_live, live_now, grad_act, gain_row):
    _, pullback = jax.vjp(lambda floats: activate(floats, gain_row), values.astype(jnp.float32))
    (through,) = pullback(grad_act)
    summed = grad_live.astype(jnp.float32) + through
    result = jnp.where(live_now[:, None], summed, jnp.zeros_like(summed))
    return result.astype(jnp.bfloat16)


def shards(segment_inputs, out_cotangent, neighbours, block_counts, norm_gain, kernel):
    n_pipe = lax.axis_size("pipe")
    n_x = lax.axis_size("sx")
    n_y = lax.axis_size("sy")
    segment_place = lax.axis_index("pipe")
    micro_count = segment_inputs.shape[1]
    row_count = segment_inputs.shape[4]
    channels = segment_inputs.shape[5]
    blocks = row_count // 512
    taps = 27
    weights = gathered(kernel[0], "sx")
    flipped = weights.reshape(3, 3, 3, channels, channels)[::-1, ::-1, ::-1].transpose(0, 1, 2, 4, 3)
    gain_row = norm_gain[0]
    inputs = segment_inputs[0, :, 0, 0]
    cotangent = out_cotangent[:, 0, 0]
    tables = neighbours[:, 0, 0]
    slot_ids = jnp.arange(row_count, dtype=jnp.int32) // 512
    live_rows = slot_ids[None, :] < block_counts[:, 0, 0][:, None]

    def cube(values):
        return values.reshape(blocks, 8, 8, 8, channels)

    grads_out = []
    kernel_total = jnp.zeros((taps * channels, channels), jnp.float32)
    for micro in range(micro_count):
        table = tables[micro]
        live_now = live_rows[micro]
        values = inputs[micro]
        activation = activate(values, gain_row).astype(jnp.bfloat16)
        start = cotangent[micro]
        start = jnp.where(live_now[:, None], start, jnp.zeros_like(start))
        both = jnp.concatenate([cube(activation), cube(start)], axis=-1)
        got = exchange(both, ("sx", "sy"), (n_x, n_y), 0)
        act_pad = assemble(cube(activation), {k: v[..., :channels] for k, v in got.items()}, table)
        centre = start
        received = {k: v[..., channels:] for k, v in got.items()}
        kept_dy = start
        kept_grad = jnp.zeros((row_count, channels), jnp.bfloat16)
        for tick in range(n_pipe):
            active = segment_place == n_pipe - 1 - tick
            grad_pad = assemble(cube(centre), received, table)
            grad_act = conv_data(grad_pad, flipped).reshape(row_count, channels)
            result = finish_grad(values, centre, live_now, grad_act, gain_row)
            kept_dy = jnp.where(active, centre, kept_dy)
            kept_grad = jnp.where(active, result, kept_grad)
            if tick < n_pipe - 1:
                down = [(p, p - 1) for p in range(1, n_pipe)]
                centre = lax.ppermute(result, "pipe", down)
                received = exchange(cube(result), ("pipe", "sx", "sy"), (n_pipe, n_x, n_y), 1)
        per_tap = conv_filter(act_pad, cube(kept_dy))
        kernel_total = kernel_total + per_tap.transpose(1, 2, 3, 0, 4).reshape(taps * channels, channels)
        grads_out.append(kept_grad)
    grad_store = jnp.stack(grads_out)
    norm_scale = float(n_x * n_y * micro_count * row_count) ** (-0.5)
    kernel_term = kernel_total * norm_scale
    shard_rows = kernel.shape[1]
    over_x = scattered_sum(kernel_term.astype(jnp.bfloat16), "sx", shard_rows)
    partner = lax.ppermute(over_x, "sy", [(i, i ^ 1) for i in range(n_y)]) if n_y == 2 else None
    if partner is not None:
        kernel_share = over_x + partner
    else:
        kernel_share = lax.psum(over_x, "sy")
    return (grad_store[None, :, None, None], kernel_share[None])


def solution(mesh):
    return jax.shard_map(
        shards,
        mesh=mesh,
        in_specs=(
            P("pipe", None, "sx", "sy", None, None),
            P(None, "sx", "sy", None, None),
            P(None, "sx", "sy", None, None),
            P(None, "sx", "sy"),
            P("pipe", None),
            P("pipe", "sx", None),
        ),
        out_specs=(P("pipe", None, "sx", "sy", None, None), P("pipe", "sx", None)),
        check_vma=False,
    )
```

```python
import jax
import jax.numpy as jnp
from jax import lax
from jax.sharding import PartitionSpec as P

OFFSETS = (-1, 0, 1)


def source_range(offset):
    if offset < 0:
        return slice(7, 8)
    if offset > 0:
        return slice(0, 1)
    return slice(0, 8)


def activate(values, gain_row):
    floats = values.astype(jnp.float32)
    square = jnp.mean(floats * floats, axis=-1, keepdims=True)
    return jax.nn.silu(floats * lax.rsqrt(square + 1e-06) * gain_row)


def with_blank(blocks_in):
    return jnp.concatenate([blocks_in, jnp.zeros_like(blocks_in)], axis=0)


def face_piece(cube, shift_x, shift_y):
    return cube[:, source_range(shift_x), source_range(shift_y)]


def directions():
    return [(sx, sy) for sx in OFFSETS for sy in OFFSETS if (sx, sy) != (0, 0)]


def assemble(centre, received, table):
    slabs_x = []
    for shift_x in OFFSETS:
        rows_y = []
        for shift_y in OFFSETS:
            column = (shift_x + 1) * 3 + (shift_y + 1)
            piece = centre if (shift_x, shift_y) == (0, 0) else received[(shift_x, shift_y)]
            source = with_blank(piece)
            parts_z = []
            for shift_z in OFFSETS:
                direction = column * 3 + shift_z + 1
                if piece.shape[0] == 1:
                    chosen = table[:, direction][:, None, None, None, None] == 0
                    picked = jnp.where(chosen, piece, jnp.zeros_like(piece))
                else:
                    picked = source[table[:, direction]]
                parts_z.append(picked[:, :, :, source_range(shift_z), :])
            rows_y.append(jnp.concatenate(parts_z, axis=3))
        slabs_x.append(jnp.concatenate(rows_y, axis=2))
    return jnp.concatenate(slabs_x, axis=1)


def exchange(cube, axes, sizes, pipe_step):
    received = {}
    for shift_x, shift_y in directions():
        piece = face_piece(cube, shift_x, shift_y)
        route = []
        if pipe_step:
            n_pipe, n_x, n_y = sizes
            for p in range(pipe_step, n_pipe):
                for a in range(n_x):
                    for b in range(n_y):
                        ta, tb = a - shift_x, b - shift_y
                        if 0 <= ta < n_x and 0 <= tb < n_y:
                            route.append(((p * n_x + a) * n_y + b, ((p - pipe_step) * n_x + ta) * n_y + tb))
        else:
            n_x, n_y = sizes
            for a in range(n_x):
                for b in range(n_y):
                    ta, tb = a - shift_x, b - shift_y
                    if 0 <= ta < n_x and 0 <= tb < n_y:
                        route.append((a * n_y + b, ta * n_y + tb))
        received[(shift_x, shift_y)] = lax.ppermute(piece, axes, route)
    return received


def conv_data(padded, filters):
    return lax.conv_general_dilated(
        padded,
        filters,
        (1, 1, 1),
        "VALID",
        dimension_numbers=("NDHWC", "DHWIO", "NDHWC"),
        preferred_element_type=jnp.float32,
    )


def conv_filter(padded, grad_cube):
    return lax.conv_general_dilated(
        padded,
        grad_cube,
        (1, 1, 1),
        "VALID",
        dimension_numbers=("CDHWN", "IDHWO", "NDHWC"),
        preferred_element_type=jnp.float32,
    )


def gathered(shard, axis):
    count = lax.axis_size(axis)
    place = lax.axis_index(axis)
    parts = [shard]
    for step in range(1, count):
        parts.append(lax.ppermute(shard, axis, [(i, (i + step) % count) for i in range(count)]))
    ordered = jnp.stack(parts)
    index = (place - jnp.arange(count)) % count
    slots = jnp.zeros((count,), jnp.int32).at[index].set(jnp.arange(count, dtype=jnp.int32))
    return ordered[slots].reshape(count * shard.shape[0], *shard.shape[1:])


def scattered_sum(full, axis, share_rows):
    count = lax.axis_size(axis)
    place = lax.axis_index(axis)
    total = lax.dynamic_slice_in_dim(full, place * share_rows, share_rows, axis=0).astype(jnp.float32)
    for step in range(1, count):
        target = (place + step) % count
        piece = lax.dynamic_slice_in_dim(full, target * share_rows, share_rows, axis=0)
        total = total + lax.ppermute(piece, axis, [(i, (i + step) % count) for i in range(count)]).astype(
            jnp.float32
        )
    return total


def finish_grad(values, grad_live, live_now, grad_act, gain_row):
    _, pullback = jax.vjp(lambda floats: activate(floats, gain_row), values.astype(jnp.float32))
    (through,) = pullback(grad_act)
    summed = grad_live.astype(jnp.float32) + through
    result = jnp.where(live_now[:, None], summed, jnp.zeros_like(summed))
    return result.astype(jnp.bfloat16)


def shards(segment_inputs, out_cotangent, neighbours, block_counts, norm_gain, kernel):
    n_pipe = lax.axis_size("pipe")
    n_x = lax.axis_size("sx")
    n_y = lax.axis_size("sy")
    segment_place = lax.axis_index("pipe")
    micro_count = segment_inputs.shape[1]
    row_count = segment_inputs.shape[4]
    channels = segment_inputs.shape[5]
    blocks = row_count // 512
    taps = 27
    weights = gathered(kernel[0], "sx")
    flipped = weights.reshape(3, 3, 3, channels, channels)[::-1, ::-1, ::-1].transpose(0, 1, 2, 4, 3)
    gain_row = norm_gain[0]
    inputs = segment_inputs[0, :, 0, 0]
    cotangent = out_cotangent[:, 0, 0]
    tables = neighbours[:, 0, 0]
    slot_ids = jnp.arange(row_count, dtype=jnp.int32) // 512
    live_rows = slot_ids[None, :] < block_counts[:, 0, 0][:, None]

    def cube(values):
        return values.reshape(blocks, 8, 8, 8, channels)

    grads_out = []
    kernel_total = jnp.zeros((taps * channels, channels), jnp.float32)
    for micro in range(micro_count):
        table = tables[micro]
        live_now = live_rows[micro]
        values = inputs[micro]
        activation = activate(values, gain_row).astype(jnp.bfloat16)
        start = cotangent[micro]
        start = jnp.where(live_now[:, None], start, jnp.zeros_like(start))
        both = jnp.concatenate([cube(activation), cube(start)], axis=-1)
        got = exchange(both, ("sx", "sy"), (n_x, n_y), 0)
        act_pad = assemble(cube(activation), {k: v[..., :channels] for k, v in got.items()}, table)
        centre = start
        received = {k: v[..., channels:] for k, v in got.items()}
        kept_dy = start
        kept_grad = jnp.zeros((row_count, channels), jnp.bfloat16)
        for tick in range(n_pipe):
            active = segment_place == n_pipe - 1 - tick
            grad_pad = assemble(cube(centre), received, table)
            grad_act = conv_data(grad_pad, flipped).reshape(row_count, channels)
            result = finish_grad(values, centre, live_now, grad_act, gain_row)
            kept_dy = jnp.where(active, centre, kept_dy)
            kept_grad = jnp.where(active, result, kept_grad)
            if tick < n_pipe - 1:
                down = [(p, p - 1) for p in range(1, n_pipe)]
                centre = lax.ppermute(result, "pipe", down)
                received = exchange(cube(result), ("pipe", "sx", "sy"), (n_pipe, n_x, n_y), 1)
        per_tap = conv_filter(act_pad, cube(kept_dy))
        kernel_total = kernel_total + per_tap.transpose(1, 2, 3, 0, 4).reshape(taps * channels, channels)
        grads_out.append(kept_grad)
    grad_store = jnp.stack(grads_out)
    norm_scale = float(n_x * n_y * micro_count * row_count) ** (-0.5)
    kernel_term = kernel_total * norm_scale
    shard_rows = kernel.shape[1]
    over_x = scattered_sum(kernel_term.astype(jnp.bfloat16), "sx", shard_rows)
    partner = lax.ppermute(over_x, "sy", [(i, i ^ 1) for i in range(n_y)]) if n_y == 2 else None
    if partner is not None:
        kernel_share = over_x + partner
    else:
        kernel_share = lax.psum(over_x, "sy")
    return (grad_store[None, :, None, None], kernel_share[None])


def solution(mesh):
    return jax.shard_map(
        shards,
        mesh=mesh,
        in_specs=(
            P("pipe", None, "sx", "sy", None, None),
            P(None, "sx", "sy", None, None),
            P(None, "sx", "sy", None, None),
            P(None, "sx", "sy"),
            P("pipe", None),
            P("pipe", "sx", None),
        ),
        out_specs=(P("pipe", None, "sx", "sy", None, None), P("pipe", "sx", None)),
        check_vma=False,
    )
```

```python
import jax
import jax.numpy as jnp
from jax import lax
from jax.sharding import PartitionSpec as P

OFFSETS = (-1, 0, 1)


def source_range(offset):
    if offset < 0:
        return slice(7, 8)
    if offset > 0:
        return slice(0, 1)
    return slice(0, 8)


def activate(values, gain_row):
    floats = values.astype(jnp.float32)
    square = jnp.mean(floats * floats, axis=-1, keepdims=True)
    return jax.nn.silu(floats * lax.rsqrt(square + 1e-06) * gain_row)


def with_blank(blocks_in):
    return jnp.concatenate([blocks_in, jnp.zeros_like(blocks_in)], axis=0)


def face_piece(cube, shift_x, shift_y):
    return cube[:, source_range(shift_x), source_range(shift_y)]


def directions():
    return [(sx, sy) for sx in OFFSETS for sy in OFFSETS if (sx, sy) != (0, 0)]


def assemble(centre, received, table):
    slabs_x = []
    for shift_x in OFFSETS:
        rows_y = []
        for shift_y in OFFSETS:
            column = (shift_x + 1) * 3 + (shift_y + 1)
            piece = centre if (shift_x, shift_y) == (0, 0) else received[(shift_x, shift_y)]
            source = with_blank(piece)
            parts_z = []
            for shift_z in OFFSETS:
                direction = column * 3 + shift_z + 1
                if piece.shape[0] == 1:
                    chosen = table[:, direction][:, None, None, None, None] == 0
                    picked = jnp.where(chosen, piece, jnp.zeros_like(piece))
                else:
                    picked = source[table[:, direction]]
                parts_z.append(picked[:, :, :, source_range(shift_z), :])
            rows_y.append(jnp.concatenate(parts_z, axis=3))
        slabs_x.append(jnp.concatenate(rows_y, axis=2))
    return jnp.concatenate(slabs_x, axis=1)


def exchange(cube, axes, sizes, pipe_step):
    n_pipe, n_x, n_y = sizes if pipe_step else (pipe_step + 1, *sizes)

    def linear(p, a, b):
        return (p * n_x + a) * n_y + b if pipe_step else a * n_y + b

    def send(piece, moves):
        route = []
        for p in range(pipe_step, n_pipe):
            for a in range(n_x):
                for b in range(n_y):
                    ta, tb = moves(a, b)
                    if 0 <= ta < n_x and 0 <= tb < n_y:
                        route.append((linear(p, a, b), linear(p - pipe_step, ta, tb)))
        return lax.ppermute(piece, axes, route)

    received = {}
    if n_y == 2:
        place_y = lax.axis_index("sy")
        for shift_x in OFFSETS:
            if shift_x != 0:
                received[(shift_x, 0)] = send(
                    face_piece(cube, shift_x, 0), lambda a, b, i=shift_x: (a - i, b)
                )
            row = lax.dynamic_slice_in_dim(cube[:, source_range(shift_x)], (1 - place_y) * 7, 1, axis=2)
            got = send(row, lambda a, b, i=shift_x: (a - i, 1 - b))
            blank = jnp.zeros_like(got)
            received[(shift_x, 1)] = jnp.where(place_y == 0, got, blank)
            received[(shift_x, -1)] = jnp.where(place_y == 1, got, blank)
        return received
    for shift_x, shift_y in directions():
        received[(shift_x, shift_y)] = send(
            face_piece(cube, shift_x, shift_y), lambda a, b, i=shift_x, j=shift_y: (a - i, b - j)
        )
    return received


def conv_data(padded, filters):
    return lax.conv_general_dilated(
        padded,
        filters,
        (1, 1, 1),
        "VALID",
        dimension_numbers=("NDHWC", "DHWIO", "NDHWC"),
        preferred_element_type=jnp.float32,
    )


def conv_filter(padded, grad_cube):
    return lax.conv_general_dilated(
        padded,
        grad_cube,
        (1, 1, 1),
        "VALID",
        dimension_numbers=("CDHWN", "IDHWO", "NDHWC"),
        preferred_element_type=jnp.float32,
    )


def gathered(shard, axis):
    count = lax.axis_size(axis)
    place = lax.axis_index(axis)
    parts = [shard]
    for step in range(1, count):
        parts.append(lax.ppermute(shard, axis, [(i, (i + step) % count) for i in range(count)]))
    ordered = jnp.stack(parts)
    index = (place - jnp.arange(count)) % count
    slots = jnp.zeros((count,), jnp.int32).at[index].set(jnp.arange(count, dtype=jnp.int32))
    return ordered[slots].reshape(count * shard.shape[0], *shard.shape[1:])


def scattered_sum(full, axis, share_rows):
    count = lax.axis_size(axis)
    place = lax.axis_index(axis)
    total = lax.dynamic_slice_in_dim(full, place * share_rows, share_rows, axis=0).astype(jnp.float32)
    for step in range(1, count):
        target = (place + step) % count
        piece = lax.dynamic_slice_in_dim(full, target * share_rows, share_rows, axis=0)
        total = total + lax.ppermute(piece, axis, [(i, (i + step) % count) for i in range(count)]).astype(
            jnp.float32
        )
    return total


def finish_grad(values, grad_live, live_now, grad_act, gain_row):
    _, pullback = jax.vjp(lambda floats: activate(floats, gain_row), values.astype(jnp.float32))
    (through,) = pullback(grad_act)
    summed = grad_live.astype(jnp.float32) + through
    result = jnp.where(live_now[:, None], summed, jnp.zeros_like(summed))
    return result.astype(jnp.bfloat16)


def shards(segment_inputs, out_cotangent, neighbours, block_counts, norm_gain, kernel):
    n_pipe = lax.axis_size("pipe")
    n_x = lax.axis_size("sx")
    n_y = lax.axis_size("sy")
    segment_place = lax.axis_index("pipe")
    micro_count = segment_inputs.shape[1]
    row_count = segment_inputs.shape[4]
    channels = segment_inputs.shape[5]
    blocks = row_count // 512
    taps = 27
    weights = gathered(kernel[0], "sx")
    flipped = weights.reshape(3, 3, 3, channels, channels)[::-1, ::-1, ::-1].transpose(0, 1, 2, 4, 3)
    gain_row = norm_gain[0]
    inputs = segment_inputs[0, :, 0, 0]
    cotangent = out_cotangent[:, 0, 0]
    tables = neighbours[:, 0, 0]
    slot_ids = jnp.arange(row_count, dtype=jnp.int32) // 512
    live_rows = slot_ids[None, :] < block_counts[:, 0, 0][:, None]

    def cube(values):
        return values.reshape(blocks, 8, 8, 8, channels)

    grads_out = []
    kernel_total = jnp.zeros((taps * channels, channels), jnp.float32)
    for micro in range(micro_count):
        table = tables[micro]
        live_now = live_rows[micro]
        values = inputs[micro]
        activation = activate(values, gain_row).astype(jnp.bfloat16)
        start = cotangent[micro]
        start = jnp.where(live_now[:, None], start, jnp.zeros_like(start))
        both = jnp.concatenate([cube(activation), cube(start)], axis=-1)
        got = exchange(both, ("sx", "sy"), (n_x, n_y), 0)
        both_pad = assemble(both, got, table)
        act_pad = both_pad[..., :channels]
        centre = start
        received = None
        kept_dy = start
        kept_grad = jnp.zeros((row_count, channels), jnp.bfloat16)
        for tick in range(n_pipe):
            active = segment_place == n_pipe - 1 - tick
            grad_pad = both_pad[..., channels:] if tick == 0 else assemble(cube(centre), received, table)
            grad_act = conv_data(grad_pad, flipped).reshape(row_count, channels)
            result = finish_grad(values, centre, live_now, grad_act, gain_row)
            kept_dy = jnp.where(active, centre, kept_dy)
            kept_grad = jnp.where(active, result, kept_grad)
            if tick < n_pipe - 1:
                down = [(p, p - 1) for p in range(1, n_pipe)]
                centre = lax.ppermute(result, "pipe", down)
                received = exchange(cube(result), ("pipe", "sx", "sy"), (n_pipe, n_x, n_y), 1)
        per_tap = conv_filter(act_pad, cube(kept_dy))
        kernel_total = kernel_total + per_tap.transpose(1, 2, 3, 0, 4).reshape(taps * channels, channels)
        grads_out.append(kept_grad)
    grad_store = jnp.stack(grads_out)
    norm_scale = float(n_x * n_y * micro_count * row_count) ** (-0.5)
    kernel_term = kernel_total * norm_scale
    shard_rows = kernel.shape[1]
    over_x = scattered_sum(kernel_term.astype(jnp.bfloat16), "sx", shard_rows)
    partner = lax.ppermute(over_x, "sy", [(i, i ^ 1) for i in range(n_y)]) if n_y == 2 else None
    if partner is not None:
        kernel_share = over_x + partner
    else:
        kernel_share = lax.psum(over_x, "sy")
    return (grad_store[None, :, None, None], kernel_share[None])


def solution(mesh):
    return jax.shard_map(
        shards,
        mesh=mesh,
        in_specs=(
            P("pipe", None, "sx", "sy", None, None),
            P(None, "sx", "sy", None, None),
            P(None, "sx", "sy", None, None),
            P(None, "sx", "sy"),
            P("pipe", None),
            P("pipe", "sx", None),
        ),
        out_specs=(P("pipe", None, "sx", "sy", None, None), P("pipe", "sx", None)),
        check_vma=False,
    )
```

```python
import jax
import jax.numpy as jnp
from jax import lax
from jax.sharding import PartitionSpec as P

OFFSETS = (-1, 0, 1)


def source_range(offset):
    if offset < 0:
        return slice(7, 8)
    if offset > 0:
        return slice(0, 1)
    return slice(0, 8)


def activate(values, gain_row):
    floats = values.astype(jnp.float32)
    square = jnp.mean(floats * floats, axis=-1, keepdims=True)
    return jax.nn.silu(floats * lax.rsqrt(square + 1e-06) * gain_row)


def with_blank(blocks_in):
    return jnp.concatenate([blocks_in, jnp.zeros_like(blocks_in)], axis=0)


def face_piece(cube, shift_x, shift_y):
    return cube[:, source_range(shift_x), source_range(shift_y)]


def directions():
    return [(sx, sy) for sx in OFFSETS for sy in OFFSETS if (sx, sy) != (0, 0)]


def assemble(centre, received, table):
    slabs_x = []
    for shift_x in OFFSETS:
        rows_y = []
        for shift_y in OFFSETS:
            column = (shift_x + 1) * 3 + (shift_y + 1)
            piece = centre if (shift_x, shift_y) == (0, 0) else received[(shift_x, shift_y)]
            source = with_blank(piece)
            parts_z = []
            for shift_z in OFFSETS:
                direction = column * 3 + shift_z + 1
                if piece.shape[0] == 1:
                    chosen = table[:, direction][:, None, None, None, None] == 0
                    picked = jnp.where(chosen, piece, jnp.zeros_like(piece))
                else:
                    picked = source[table[:, direction]]
                parts_z.append(picked[:, :, :, source_range(shift_z), :])
            rows_y.append(jnp.concatenate(parts_z, axis=3))
        slabs_x.append(jnp.concatenate(rows_y, axis=2))
    return jnp.concatenate(slabs_x, axis=1)


def exchange(cube, axes, sizes, pipe_step):
    n_pipe, n_x, n_y = sizes if pipe_step else (pipe_step + 1, *sizes)

    def linear(p, a, b):
        return (p * n_x + a) * n_y + b if pipe_step else a * n_y + b

    def send(piece, moves):
        route = []
        for p in range(pipe_step, n_pipe):
            for a in range(n_x):
                for b in range(n_y):
                    ta, tb = moves(a, b)
                    if 0 <= ta < n_x and 0 <= tb < n_y:
                        route.append((linear(p, a, b), linear(p - pipe_step, ta, tb)))
        return lax.ppermute(piece, axes, route)

    received = {}
    if n_y == 2:
        place_y = lax.axis_index("sy")
        for shift_x in OFFSETS:
            if shift_x != 0:
                received[(shift_x, 0)] = send(
                    face_piece(cube, shift_x, 0), lambda a, b, i=shift_x: (a - i, b)
                )
            row = lax.dynamic_slice_in_dim(cube[:, source_range(shift_x)], (1 - place_y) * 7, 1, axis=2)
            got = send(row, lambda a, b, i=shift_x: (a - i, 1 - b))
            blank = jnp.zeros_like(got)
            received[(shift_x, 1)] = jnp.where(place_y == 0, got, blank)
            received[(shift_x, -1)] = jnp.where(place_y == 1, got, blank)
        return received
    for shift_x, shift_y in directions():
        received[(shift_x, shift_y)] = send(
            face_piece(cube, shift_x, shift_y), lambda a, b, i=shift_x, j=shift_y: (a - i, b - j)
        )
    return received


def conv_data(padded, filters):
    return lax.conv_general_dilated(
        padded,
        filters,
        (1, 1, 1),
        "VALID",
        dimension_numbers=("NDHWC", "DHWIO", "NDHWC"),
        preferred_element_type=jnp.float32,
    )


def conv_filter(padded, grad_cube):
    return lax.conv_general_dilated(
        padded,
        grad_cube,
        (1, 1, 1),
        "VALID",
        dimension_numbers=("CDHWN", "IDHWO", "NDHWC"),
        preferred_element_type=jnp.float32,
    )


def gathered(shard, axis):
    count = lax.axis_size(axis)
    place = lax.axis_index(axis)
    parts = [shard]
    rows = shard.shape[0]
    if lax.axis_size("sy") == 2 and rows % 2 == 0:
        half = rows // 2
        place_y = lax.axis_index("sy")
        mine = lax.dynamic_slice_in_dim(shard, place_y * half, half, axis=0)
        fetched = jnp.stack(
            [lax.ppermute(mine, axis, [(i, (i + step) % count) for i in range(count)]) for step in range(1, count)]
        )
        other = lax.ppermute(fetched, "sy", [(0, 1), (1, 0)])
        low = jnp.where(place_y == 0, fetched, other)
        high = jnp.where(place_y == 0, other, fetched)
        remote = jnp.concatenate([low, high], axis=1)
        parts.extend(remote[step - 1] for step in range(1, count))
    else:
        for step in range(1, count):
            parts.append(lax.ppermute(shard, axis, [(i, (i + step) % count) for i in range(count)]))
    ordered = jnp.stack(parts)
    index = (place - jnp.arange(count)) % count
    slots = jnp.zeros((count,), jnp.int32).at[index].set(jnp.arange(count, dtype=jnp.int32))
    return ordered[slots].reshape(count * shard.shape[0], *shard.shape[1:])


def scattered_sum(full, axis, share_rows):
    count = lax.axis_size(axis)
    place = lax.axis_index(axis)
    total = lax.dynamic_slice_in_dim(full, place * share_rows, share_rows, axis=0).astype(jnp.float32)
    for step in range(1, count):
        target = (place + step) % count
        piece = lax.dynamic_slice_in_dim(full, target * share_rows, share_rows, axis=0)
        total = total + lax.ppermute(piece, axis, [(i, (i + step) % count) for i in range(count)]).astype(
            jnp.float32
        )
    return total


def finish_grad(values, grad_live, live_now, grad_act, gain_row):
    _, pullback = jax.vjp(lambda floats: activate(floats, gain_row), values.astype(jnp.float32))
    (through,) = pullback(grad_act)
    summed = grad_live.astype(jnp.float32) + through
    result = jnp.where(live_now[:, None], summed, jnp.zeros_like(summed))
    return result.astype(jnp.bfloat16)


def shards(segment_inputs, out_cotangent, neighbours, block_counts, norm_gain, kernel):
    n_pipe = lax.axis_size("pipe")
    n_x = lax.axis_size("sx")
    n_y = lax.axis_size("sy")
    segment_place = lax.axis_index("pipe")
    micro_count = segment_inputs.shape[1]
    row_count = segment_inputs.shape[4]
    channels = segment_inputs.shape[5]
    blocks = row_count // 512
    taps = 27
    weights = gathered(kernel[0], "sx")
    flipped = weights.reshape(3, 3, 3, channels, channels)[::-1, ::-1, ::-1].transpose(0, 1, 2, 4, 3)
    gain_row = norm_gain[0]
    inputs = segment_inputs[0, :, 0, 0]
    cotangent = out_cotangent[:, 0, 0]
    tables = neighbours[:, 0, 0]
    slot_ids = jnp.arange(row_count, dtype=jnp.int32) // 512
    live_rows = slot_ids[None, :] < block_counts[:, 0, 0][:, None]

    def cube(values):
        return values.reshape(blocks, 8, 8, 8, channels)

    grads_out = []
    kernel_total = jnp.zeros((taps * channels, channels), jnp.float32)
    for micro in range(micro_count):
        table = tables[micro]
        live_now = live_rows[micro]
        values = inputs[micro]
        activation = activate(values, gain_row).astype(jnp.bfloat16)
        start = cotangent[micro]
        start = jnp.where(live_now[:, None], start, jnp.zeros_like(start))
        both = jnp.concatenate([cube(activation), cube(start)], axis=-1)
        got = exchange(both, ("sx", "sy"), (n_x, n_y), 0)
        both_pad = assemble(both, got, table)
        act_pad = both_pad[..., :channels]
        centre = start
        received = None
        kept_dy = start
        kept_grad = jnp.zeros((row_count, channels), jnp.bfloat16)
        for tick in range(n_pipe):
            active = segment_place == n_pipe - 1 - tick
            grad_pad = both_pad[..., channels:] if tick == 0 else assemble(cube(centre), received, table)
            grad_act = conv_data(grad_pad, flipped).reshape(row_count, channels)
            result = finish_grad(values, centre, live_now, grad_act, gain_row)
            kept_dy = jnp.where(active, centre, kept_dy)
            kept_grad = jnp.where(active, result, kept_grad)
            if tick < n_pipe - 1:
                down = [(p, p - 1) for p in range(1, n_pipe)]
                centre = lax.ppermute(result, "pipe", down)
                received = exchange(cube(result), ("pipe", "sx", "sy"), (n_pipe, n_x, n_y), 1)
        per_tap = conv_filter(act_pad, cube(kept_dy))
        kernel_total = kernel_total + per_tap.transpose(1, 2, 3, 0, 4).reshape(taps * channels, channels)
        grads_out.append(kept_grad)
    grad_store = jnp.stack(grads_out)
    norm_scale = float(n_x * n_y * micro_count * row_count) ** (-0.5)
    kernel_term = kernel_total * norm_scale
    shard_rows = kernel.shape[1]
    over_x = scattered_sum(kernel_term.astype(jnp.bfloat16), "sx", shard_rows)
    partner = lax.ppermute(over_x, "sy", [(i, i ^ 1) for i in range(n_y)]) if n_y == 2 else None
    if partner is not None:
        kernel_share = over_x + partner
    else:
        kernel_share = lax.psum(over_x, "sy")
    return (grad_store[None, :, None, None], kernel_share[None])


def solution(mesh):
    return jax.shard_map(
        shards,
        mesh=mesh,
        in_specs=(
            P("pipe", None, "sx", "sy", None, None),
            P(None, "sx", "sy", None, None),
            P(None, "sx", "sy", None, None),
            P(None, "sx", "sy"),
            P("pipe", None),
            P("pipe", "sx", None),
        ),
        out_specs=(P("pipe", None, "sx", "sy", None, None), P("pipe", "sx", None)),
        check_vma=False,
    )
```

```python
import jax
import jax.numpy as jnp
from jax import lax
from jax.sharding import PartitionSpec as P

OFFSETS = (-1, 0, 1)


def source_range(offset):
    if offset < 0:
        return slice(7, 8)
    if offset > 0:
        return slice(0, 1)
    return slice(0, 8)


def activate(values, gain_row):
    floats = values.astype(jnp.float32)
    square = jnp.mean(floats * floats, axis=-1, keepdims=True)
    return jax.nn.silu(floats * lax.rsqrt(square + 1e-06) * gain_row)


def with_blank(blocks_in):
    return jnp.concatenate([blocks_in, jnp.zeros_like(blocks_in)], axis=0)


def face_piece(cube, shift_x, shift_y):
    return cube[:, source_range(shift_x), source_range(shift_y)]


def directions():
    return [(sx, sy) for sx in OFFSETS for sy in OFFSETS if (sx, sy) != (0, 0)]


def assemble(centre, received, table):
    slabs_x = []
    for shift_x in OFFSETS:
        rows_y = []
        for shift_y in OFFSETS:
            column = (shift_x + 1) * 3 + (shift_y + 1)
            piece = centre if (shift_x, shift_y) == (0, 0) else received[(shift_x, shift_y)]
            source = with_blank(piece)
            parts_z = []
            for shift_z in OFFSETS:
                direction = column * 3 + shift_z + 1
                if piece.shape[0] == 1:
                    chosen = table[:, direction][:, None, None, None, None] == 0
                    picked = jnp.where(chosen, piece, jnp.zeros_like(piece))
                else:
                    picked = source[table[:, direction]]
                parts_z.append(picked[:, :, :, source_range(shift_z), :])
            rows_y.append(jnp.concatenate(parts_z, axis=3))
        slabs_x.append(jnp.concatenate(rows_y, axis=2))
    return jnp.concatenate(slabs_x, axis=1)


def exchange(cube, axes, sizes, pipe_step):
    n_pipe, n_x, n_y = sizes if pipe_step else (pipe_step + 1, *sizes)

    def linear(p, a, b):
        return (p * n_x + a) * n_y + b if pipe_step else a * n_y + b

    def send(piece, moves):
        route = []
        for p in range(pipe_step, n_pipe):
            for a in range(n_x):
                for b in range(n_y):
                    ta, tb = moves(a, b)
                    if 0 <= ta < n_x and 0 <= tb < n_y:
                        route.append((linear(p, a, b), linear(p - pipe_step, ta, tb)))
        return lax.ppermute(piece, axes, route)

    received = {}
    if n_y == 2:
        place_y = lax.axis_index("sy")
        for shift_x in OFFSETS:
            if shift_x != 0:
                received[(shift_x, 0)] = send(
                    face_piece(cube, shift_x, 0), lambda a, b, i=shift_x: (a - i, b)
                )
            row = lax.dynamic_slice_in_dim(cube[:, source_range(shift_x)], (1 - place_y) * 7, 1, axis=2)
            got = send(row, lambda a, b, i=shift_x: (a - i, 1 - b))
            blank = jnp.zeros_like(got)
            received[(shift_x, 1)] = jnp.where(place_y == 0, got, blank)
            received[(shift_x, -1)] = jnp.where(place_y == 1, got, blank)
        return received
    for shift_x, shift_y in directions():
        received[(shift_x, shift_y)] = send(
            face_piece(cube, shift_x, shift_y), lambda a, b, i=shift_x, j=shift_y: (a - i, b - j)
        )
    return received


def conv_data(padded, filters):
    return lax.conv_general_dilated(
        padded,
        filters,
        (1, 1, 1),
        "VALID",
        dimension_numbers=("NDHWC", "DHWIO", "NDHWC"),
        preferred_element_type=jnp.float32,
    )


def conv_filter(padded, grad_cube):
    return lax.conv_general_dilated(
        padded,
        grad_cube,
        (1, 1, 1),
        "VALID",
        dimension_numbers=("CDHWN", "IDHWO", "NDHWC"),
        preferred_element_type=jnp.float32,
    )


def gathered(shard, axis):
    count = lax.axis_size(axis)
    place = lax.axis_index(axis)
    parts = [shard]
    for step in range(1, count):
        parts.append(lax.ppermute(shard, axis, [(i, (i + step) % count) for i in range(count)]))
    ordered = jnp.stack(parts)
    index = (place - jnp.arange(count)) % count
    slots = jnp.zeros((count,), jnp.int32).at[index].set(jnp.arange(count, dtype=jnp.int32))
    return ordered[slots].reshape(count * shard.shape[0], *shard.shape[1:])


def scattered_sum(full, axis, share_rows):
    count = lax.axis_size(axis)
    place = lax.axis_index(axis)
    total = lax.dynamic_slice_in_dim(full, place * share_rows, share_rows, axis=0).astype(jnp.float32)
    for step in range(1, count):
        target = (place + step) % count
        piece = lax.dynamic_slice_in_dim(full, target * share_rows, share_rows, axis=0)
        total = total + lax.ppermute(piece, axis, [(i, (i + step) % count) for i in range(count)]).astype(
            jnp.float32
        )
    return total


def finish_grad(values, grad_live, live_now, grad_act, gain_row):
    _, pullback = jax.vjp(lambda floats: activate(floats, gain_row), values.astype(jnp.float32))
    (through,) = pullback(grad_act)
    summed = grad_live.astype(jnp.float32) + through
    result = jnp.where(live_now[:, None], summed, jnp.zeros_like(summed))
    return result.astype(jnp.bfloat16)


def shards(segment_inputs, out_cotangent, neighbours, block_counts, norm_gain, kernel):
    n_pipe = lax.axis_size("pipe")
    n_x = lax.axis_size("sx")
    n_y = lax.axis_size("sy")
    segment_place = lax.axis_index("pipe")
    micro_count = segment_inputs.shape[1]
    row_count = segment_inputs.shape[4]
    channels = segment_inputs.shape[5]
    blocks = row_count // 512
    taps = 27
    weights = gathered(kernel[0], "sx")
    flipped = weights.reshape(3, 3, 3, channels, channels)[::-1, ::-1, ::-1].transpose(0, 1, 2, 4, 3)
    gain_row = norm_gain[0]
    inputs = segment_inputs[0, :, 0, 0]
    cotangent = out_cotangent[:, 0, 0]
    tables = neighbours[:, 0, 0]
    slot_ids = jnp.arange(row_count, dtype=jnp.int32) // 512
    live_rows = slot_ids[None, :] < block_counts[:, 0, 0][:, None]

    def cube(values):
        return values.reshape(blocks, 8, 8, 8, channels)

    grads_out = []
    kernel_total = jnp.zeros((taps * channels, channels), jnp.float32)
    norm_scale = float(n_x * n_y * micro_count * row_count) ** (-0.5)
    shard_rows = kernel.shape[1]
    kernel_term = None
    for micro in range(micro_count):
        table = tables[micro]
        live_now = live_rows[micro]
        values = inputs[micro]
        activation = activate(values, gain_row).astype(jnp.bfloat16)
        start = cotangent[micro]
        start = jnp.where(live_now[:, None], start, jnp.zeros_like(start))
        both = jnp.concatenate([cube(activation), cube(start)], axis=-1)
        got = exchange(both, ("sx", "sy"), (n_x, n_y), 0)
        both_pad = assemble(both, got, table)
        act_pad = both_pad[..., :channels]
        centre = start
        received = None
        kept_dy = start
        kept_grad = jnp.zeros((row_count, channels), jnp.bfloat16)
        for tick in range(n_pipe):
            active = segment_place == n_pipe - 1 - tick
            kept_dy = jnp.where(active, centre, kept_dy)
            if tick == n_pipe - 1:
                per_tap = conv_filter(act_pad, cube(kept_dy))
                kernel_total = kernel_total + per_tap.transpose(1, 2, 3, 0, 4).reshape(taps * channels, channels)
                if micro == micro_count - 1:
                    kernel_term = (kernel_total * norm_scale).astype(jnp.bfloat16)
                    kernel_term, centre, received, both_pad = lax.optimization_barrier(
                        (kernel_term, centre, received, both_pad)
                    )
            grad_pad = both_pad[..., channels:] if tick == 0 else assemble(cube(centre), received, table)
            grad_act = conv_data(grad_pad, flipped).reshape(row_count, channels)
            result = finish_grad(values, centre, live_now, grad_act, gain_row)
            kept_grad = jnp.where(active, result, kept_grad)
            if tick < n_pipe - 1:
                down = [(p, p - 1) for p in range(1, n_pipe)]
                centre = lax.ppermute(result, "pipe", down)
                received = exchange(cube(result), ("pipe", "sx", "sy"), (n_pipe, n_x, n_y), 1)
        grads_out.append(kept_grad)
    grad_store = jnp.stack(grads_out)
    over_x = scattered_sum(kernel_term, "sx", shard_rows)
    partner = lax.ppermute(over_x, "sy", [(i, i ^ 1) for i in range(n_y)]) if n_y == 2 else None
    if partner is not None:
        kernel_share = over_x + partner
    else:
        kernel_share = lax.psum(over_x, "sy")
    return (grad_store[None, :, None, None], kernel_share[None])


def solution(mesh):
    return jax.shard_map(
        shards,
        mesh=mesh,
        in_specs=(
            P("pipe", None, "sx", "sy", None, None),
            P(None, "sx", "sy", None, None),
            P(None, "sx", "sy", None, None),
            P(None, "sx", "sy"),
            P("pipe", None),
            P("pipe", "sx", None),
        ),
        out_specs=(P("pipe", None, "sx", "sy", None, None), P("pipe", "sx", None)),
        check_vma=False,
    )
```

```python
import jax
import jax.numpy as jnp
from jax import lax
from jax.sharding import PartitionSpec as P

OFFSETS = (-1, 0, 1)


def source_range(offset):
    if offset < 0:
        return slice(7, 8)
    if offset > 0:
        return slice(0, 1)
    return slice(0, 8)


def activate(values, gain_row):
    floats = values.astype(jnp.float32)
    square = jnp.mean(floats * floats, axis=-1, keepdims=True)
    return jax.nn.silu(floats * lax.rsqrt(square + 1e-06) * gain_row)


def with_blank(blocks_in):
    return jnp.concatenate([blocks_in, jnp.zeros_like(blocks_in)], axis=0)


def face_piece(cube, shift_x, shift_y):
    return cube[:, source_range(shift_x), source_range(shift_y)]


def directions():
    return [(sx, sy) for sx in OFFSETS for sy in OFFSETS if (sx, sy) != (0, 0)]


def assemble(centre, received, table):
    slabs_x = []
    for shift_x in OFFSETS:
        rows_y = []
        for shift_y in OFFSETS:
            column = (shift_x + 1) * 3 + (shift_y + 1)
            piece = centre if (shift_x, shift_y) == (0, 0) else received[(shift_x, shift_y)]
            source = with_blank(piece)
            parts_z = []
            for shift_z in OFFSETS:
                direction = column * 3 + shift_z + 1
                if piece.shape[0] == 1:
                    chosen = table[:, direction][:, None, None, None, None] == 0
                    picked = jnp.where(chosen, piece, jnp.zeros_like(piece))
                else:
                    picked = source[table[:, direction]]
                parts_z.append(picked[:, :, :, source_range(shift_z), :])
            rows_y.append(jnp.concatenate(parts_z, axis=3))
        slabs_x.append(jnp.concatenate(rows_y, axis=2))
    return jnp.concatenate(slabs_x, axis=1)


def exchange(cube, axes, sizes, pipe_step, carry=None, carried=None):
    n_pipe, n_x, n_y = sizes if pipe_step else (pipe_step + 1, *sizes)

    def linear(p, a, b):
        return (p * n_x + a) * n_y + b if pipe_step else a * n_y + b

    def send(piece, moves):
        route = []
        for p in range(pipe_step, n_pipe):
            for a in range(n_x):
                for b in range(n_y):
                    ta, tb = moves(a, b)
                    if 0 <= ta < n_x and 0 <= tb < n_y:
                        route.append((linear(p, a, b), linear(p - pipe_step, ta, tb)))
        return lax.ppermute(piece, axes, route)

    def face_x(shift_x):
        face = face_piece(cube, shift_x, 0)
        if carry is None:
            return send(face, lambda a, b: (a - shift_x, b))
        rows = carry.shape[-1]
        payload = jnp.concatenate([carry, face.reshape(-1, rows)], axis=0)
        got = send(payload, lambda a, b: ((a - shift_x) % n_x, b))
        carried[(-shift_x) % n_x] = got[: carry.shape[0]]
        return got[carry.shape[0] :].reshape(face.shape)

    received = {}
    if n_y == 2:
        place_y = lax.axis_index("sy")
        for shift_x in OFFSETS:
            if shift_x != 0:
                received[(shift_x, 0)] = face_x(shift_x)
            row = lax.dynamic_slice_in_dim(cube[:, source_range(shift_x)], (1 - place_y) * 7, 1, axis=2)
            got = send(row, lambda a, b, i=shift_x: (a - i, 1 - b))
            blank = jnp.zeros_like(got)
            received[(shift_x, 1)] = jnp.where(place_y == 0, got, blank)
            received[(shift_x, -1)] = jnp.where(place_y == 1, got, blank)
        return received
    for shift_x, shift_y in directions():
        if shift_y == 0:
            received[(shift_x, 0)] = face_x(shift_x)
            continue
        received[(shift_x, shift_y)] = send(
            face_piece(cube, shift_x, shift_y), lambda a, b, i=shift_x, j=shift_y: (a - i, b - j)
        )
    return received


def conv_data(padded, filters):
    return lax.conv_general_dilated(
        padded,
        filters,
        (1, 1, 1),
        "VALID",
        dimension_numbers=("NDHWC", "DHWIO", "NDHWC"),
        preferred_element_type=jnp.float32,
    )


def conv_filter(padded, grad_cube):
    return lax.conv_general_dilated(
        padded,
        grad_cube,
        (1, 1, 1),
        "VALID",
        dimension_numbers=("CDHWN", "IDHWO", "NDHWC"),
        preferred_element_type=jnp.float32,
    )


def gathered(shard, axis, given):
    count = lax.axis_size(axis)
    place = lax.axis_index(axis)
    parts = [shard]
    for step in range(1, count):
        if step in given:
            parts.append(given[step])
        else:
            parts.append(lax.ppermute(shard, axis, [(i, (i + step) % count) for i in range(count)]))
    ordered = jnp.stack(parts)
    index = (place - jnp.arange(count)) % count
    slots = jnp.zeros((count,), jnp.int32).at[index].set(jnp.arange(count, dtype=jnp.int32))
    return ordered[slots].reshape(count * shard.shape[0], *shard.shape[1:])


def scattered_sum(full, axis, share_rows):
    count = lax.axis_size(axis)
    place = lax.axis_index(axis)
    total = lax.dynamic_slice_in_dim(full, place * share_rows, share_rows, axis=0).astype(jnp.float32)
    for step in range(1, count):
        target = (place + step) % count
        piece = lax.dynamic_slice_in_dim(full, target * share_rows, share_rows, axis=0)
        total = total + lax.ppermute(piece, axis, [(i, (i + step) % count) for i in range(count)]).astype(
            jnp.float32
        )
    return total


def finish_grad(values, grad_live, live_now, grad_act, gain_row):
    _, pullback = jax.vjp(lambda floats: activate(floats, gain_row), values.astype(jnp.float32))
    (through,) = pullback(grad_act)
    summed = grad_live.astype(jnp.float32) + through
    result = jnp.where(live_now[:, None], summed, jnp.zeros_like(summed))
    return result.astype(jnp.bfloat16)


def shards(segment_inputs, out_cotangent, neighbours, block_counts, norm_gain, kernel):
    n_pipe = lax.axis_size("pipe")
    n_x = lax.axis_size("sx")
    n_y = lax.axis_size("sy")
    segment_place = lax.axis_index("pipe")
    micro_count = segment_inputs.shape[1]
    row_count = segment_inputs.shape[4]
    channels = segment_inputs.shape[5]
    blocks = row_count // 512
    taps = 27
    gain_row = norm_gain[0]
    inputs = segment_inputs[0, :, 0, 0]
    cotangent = out_cotangent[:, 0, 0]
    tables = neighbours[:, 0, 0]
    slot_ids = jnp.arange(row_count, dtype=jnp.int32) // 512
    live_rows = slot_ids[None, :] < block_counts[:, 0, 0][:, None]

    def cube(values):
        return values.reshape(blocks, 8, 8, 8, channels)

    grads_out = []
    kernel_total = jnp.zeros((taps * channels, channels), jnp.float32)
    norm_scale = float(n_x * n_y * micro_count * row_count) ** (-0.5)
    shard_rows = kernel.shape[1]
    kernel_term = None
    for micro in range(micro_count):
        table = tables[micro]
        live_now = live_rows[micro]
        values = inputs[micro]
        activation = activate(values, gain_row).astype(jnp.bfloat16)
        start = cotangent[micro]
        start = jnp.where(live_now[:, None], start, jnp.zeros_like(start))
        both = jnp.concatenate([cube(activation), cube(start)], axis=-1)
        if micro == 0:
            carried = {}
            riding = kernel[0] if n_x >= 3 else None
            got = exchange(both, ("sx", "sy"), (n_x, n_y), 0, riding, carried)
            weights = gathered(kernel[0], "sx", carried)
            flipped = weights.reshape(3, 3, 3, channels, channels)[::-1, ::-1, ::-1].transpose(0, 1, 2, 4, 3)
        else:
            got = exchange(both, ("sx", "sy"), (n_x, n_y), 0)
        both_pad = assemble(both, got, table)
        act_pad = both_pad[..., :channels]
        centre = start
        received = None
        kept_dy = start
        kept_grad = jnp.zeros((row_count, channels), jnp.bfloat16)
        for tick in range(n_pipe):
            active = segment_place == n_pipe - 1 - tick
            kept_dy = jnp.where(active, centre, kept_dy)
            if tick == n_pipe - 1:
                per_tap = conv_filter(act_pad, cube(kept_dy))
                kernel_total = kernel_total + per_tap.transpose(1, 2, 3, 0, 4).reshape(taps * channels, channels)
                if micro == micro_count - 1:
                    kernel_term = (kernel_total * norm_scale).astype(jnp.bfloat16)
                    kernel_term, centre, received, both_pad = lax.optimization_barrier(
                        (kernel_term, centre, received, both_pad)
                    )
            grad_pad = both_pad[..., channels:] if tick == 0 else assemble(cube(centre), received, table)
            grad_act = conv_data(grad_pad, flipped).reshape(row_count, channels)
            result = finish_grad(values, centre, live_now, grad_act, gain_row)
            kept_grad = jnp.where(active, result, kept_grad)
            if tick < n_pipe - 1:
                down = [(p, p - 1) for p in range(1, n_pipe)]
                centre = lax.ppermute(result, "pipe", down)
                received = exchange(cube(result), ("pipe", "sx", "sy"), (n_pipe, n_x, n_y), 1)
        grads_out.append(kept_grad)
    grad_store = jnp.stack(grads_out)
    over_x = scattered_sum(kernel_term, "sx", shard_rows)
    partner = lax.ppermute(over_x, "sy", [(i, i ^ 1) for i in range(n_y)]) if n_y == 2 else None
    if partner is not None:
        kernel_share = over_x + partner
    else:
        kernel_share = lax.psum(over_x, "sy")
    return (grad_store[None, :, None, None], kernel_share[None])


def solution(mesh):
    return jax.shard_map(
        shards,
        mesh=mesh,
        in_specs=(
            P("pipe", None, "sx", "sy", None, None),
            P(None, "sx", "sy", None, None),
            P(None, "sx", "sy", None, None),
            P(None, "sx", "sy"),
            P("pipe", None),
            P("pipe", "sx", None),
        ),
        out_specs=(P("pipe", None, "sx", "sy", None, None), P("pipe", "sx", None)),
        check_vma=False,
    )
```

```python
import jax
import jax.numpy as jnp
from jax import lax
from jax.sharding import PartitionSpec as P

OFFSETS = (-1, 0, 1)


def source_range(offset):
    if offset < 0:
        return slice(7, 8)
    if offset > 0:
        return slice(0, 1)
    return slice(0, 8)


def activate(values, gain_row):
    floats = values.astype(jnp.float32)
    square = jnp.mean(floats * floats, axis=-1, keepdims=True)
    return jax.nn.silu(floats * lax.rsqrt(square + 1e-06) * gain_row)


def with_blank(blocks_in):
    return jnp.concatenate([blocks_in, jnp.zeros_like(blocks_in)], axis=0)


def face_piece(cube, shift_x, shift_y):
    return cube[:, source_range(shift_x), source_range(shift_y)]


def directions():
    return [(sx, sy) for sx in OFFSETS for sy in OFFSETS if (sx, sy) != (0, 0)]


def assemble(centre, received, table, split=False):
    slabs_x = []
    for shift_x in OFFSETS:
        rows_y = []
        for shift_y in OFFSETS:
            column = (shift_x + 1) * 3 + (shift_y + 1)
            piece = centre if (shift_x, shift_y) == (0, 0) else received[(shift_x, shift_y)]
            source = with_blank(piece)
            parts_z = []
            for shift_z in OFFSETS:
                direction = column * 3 + shift_z + 1
                if piece.shape[0] == 1:
                    chosen = table[:, direction][:, None, None, None, None] == 0
                    picked = jnp.where(chosen, piece, jnp.zeros_like(piece))
                else:
                    picked = source[table[:, direction]]
                parts_z.append(picked[:, :, :, source_range(shift_z), :])
            rows_y.append(jnp.concatenate(parts_z, axis=3))
        slabs_x.append(jnp.concatenate(rows_y, axis=2))
    if split:
        slabs_x[0], slabs_x[2] = lax.optimization_barrier((slabs_x[0], slabs_x[2]))
    return jnp.concatenate(slabs_x, axis=1)


def exchange(cube, axes, sizes, pipe_step, carry=None, carried=None):
    n_pipe, n_x, n_y = sizes if pipe_step else (pipe_step + 1, *sizes)

    def linear(p, a, b):
        return (p * n_x + a) * n_y + b if pipe_step else a * n_y + b

    def send(piece, moves):
        route = []
        for p in range(pipe_step, n_pipe):
            for a in range(n_x):
                for b in range(n_y):
                    ta, tb = moves(a, b)
                    if 0 <= ta < n_x and 0 <= tb < n_y:
                        route.append((linear(p, a, b), linear(p - pipe_step, ta, tb)))
        return lax.ppermute(piece, axes, route)

    def face_x(shift_x):
        face = face_piece(cube, shift_x, 0)
        if carry is None:
            return send(face, lambda a, b: (a - shift_x, b))
        rows = carry.shape[-1]
        payload = jnp.concatenate([carry, face.reshape(-1, rows)], axis=0)
        got = send(payload, lambda a, b: ((a - shift_x) % n_x, b))
        carried[(-shift_x) % n_x] = got[: carry.shape[0]]
        return got[carry.shape[0] :].reshape(face.shape)

    received = {}
    if n_y == 2:
        place_y = lax.axis_index("sy")
        for shift_x in OFFSETS:
            if shift_x != 0:
                received[(shift_x, 0)] = face_x(shift_x)
            row = lax.dynamic_slice_in_dim(cube[:, source_range(shift_x)], (1 - place_y) * 7, 1, axis=2)
            got = send(row, lambda a, b, i=shift_x: (a - i, 1 - b))
            blank = jnp.zeros_like(got)
            received[(shift_x, 1)] = jnp.where(place_y == 0, got, blank)
            received[(shift_x, -1)] = jnp.where(place_y == 1, got, blank)
        return received
    for shift_x, shift_y in directions():
        if shift_y == 0:
            received[(shift_x, 0)] = face_x(shift_x)
            continue
        received[(shift_x, shift_y)] = send(
            face_piece(cube, shift_x, shift_y), lambda a, b, i=shift_x, j=shift_y: (a - i, b - j)
        )
    return received


def conv_data(padded, filters):
    return lax.conv_general_dilated(
        padded,
        filters,
        (1, 1, 1),
        "VALID",
        dimension_numbers=("NDHWC", "DHWIO", "NDHWC"),
        preferred_element_type=jnp.float32,
    )


def conv_filter(padded, grad_cube):
    return lax.conv_general_dilated(
        padded,
        grad_cube,
        (1, 1, 1),
        "VALID",
        dimension_numbers=("CDHWN", "IDHWO", "NDHWC"),
        preferred_element_type=jnp.float32,
    )


def gathered(shard, axis, given):
    count = lax.axis_size(axis)
    place = lax.axis_index(axis)
    parts = [shard]
    for step in range(1, count):
        if step in given:
            parts.append(given[step])
        else:
            parts.append(lax.ppermute(shard, axis, [(i, (i + step) % count) for i in range(count)]))
    ordered = jnp.stack(parts)
    index = (place - jnp.arange(count)) % count
    slots = jnp.zeros((count,), jnp.int32).at[index].set(jnp.arange(count, dtype=jnp.int32))
    return ordered[slots].reshape(count * shard.shape[0], *shard.shape[1:])


def scattered_sum(full, axis, share_rows):
    count = lax.axis_size(axis)
    place = lax.axis_index(axis)
    total = lax.dynamic_slice_in_dim(full, place * share_rows, share_rows, axis=0).astype(jnp.float32)
    for step in range(1, count):
        target = (place + step) % count
        piece = lax.dynamic_slice_in_dim(full, target * share_rows, share_rows, axis=0)
        total = total + lax.ppermute(piece, axis, [(i, (i + step) % count) for i in range(count)]).astype(
            jnp.float32
        )
    return total


def finish_grad(values, grad_live, live_now, grad_act, gain_row):
    _, pullback = jax.vjp(lambda floats: activate(floats, gain_row), values.astype(jnp.float32))
    (through,) = pullback(grad_act)
    summed = grad_live.astype(jnp.float32) + through
    result = jnp.where(live_now[:, None], summed, jnp.zeros_like(summed))
    return result.astype(jnp.bfloat16)


def shards(segment_inputs, out_cotangent, neighbours, block_counts, norm_gain, kernel):
    n_pipe = lax.axis_size("pipe")
    n_x = lax.axis_size("sx")
    n_y = lax.axis_size("sy")
    segment_place = lax.axis_index("pipe")
    micro_count = segment_inputs.shape[1]
    row_count = segment_inputs.shape[4]
    channels = segment_inputs.shape[5]
    blocks = row_count // 512
    taps = 27
    gain_row = norm_gain[0]
    inputs = segment_inputs[0, :, 0, 0]
    cotangent = out_cotangent[:, 0, 0]
    tables = neighbours[:, 0, 0]
    slot_ids = jnp.arange(row_count, dtype=jnp.int32) // 512
    live_rows = slot_ids[None, :] < block_counts[:, 0, 0][:, None]

    def cube(values):
        return values.reshape(blocks, 8, 8, 8, channels)

    grads_out = []
    kernel_total = jnp.zeros((taps * channels, channels), jnp.float32)
    norm_scale = float(n_x * n_y * micro_count * row_count) ** (-0.5)
    shard_rows = kernel.shape[1]
    kernel_term = None
    for micro in range(micro_count):
        table = tables[micro]
        live_now = live_rows[micro]
        values = inputs[micro]
        activation = activate(values, gain_row).astype(jnp.bfloat16)
        start = cotangent[micro]
        start = jnp.where(live_now[:, None], start, jnp.zeros_like(start))
        both = jnp.concatenate([cube(activation), cube(start)], axis=-1)
        if micro == 0:
            carried = {}
            riding = kernel[0] if n_x >= 3 else None
            got = exchange(both, ("sx", "sy"), (n_x, n_y), 0, riding, carried)
            weights = gathered(kernel[0], "sx", carried)
            flipped = weights.reshape(3, 3, 3, channels, channels)[::-1, ::-1, ::-1].transpose(0, 1, 2, 4, 3)
        else:
            got = exchange(both, ("sx", "sy"), (n_x, n_y), 0)
        both_pad = assemble(both, got, table, split=True)
        act_pad = both_pad[..., :channels]
        centre = start
        received = None
        kept_dy = start
        kept_grad = jnp.zeros((row_count, channels), jnp.bfloat16)
        for tick in range(n_pipe):
            active = segment_place == n_pipe - 1 - tick
            kept_dy = jnp.where(active, centre, kept_dy)
            if tick == n_pipe - 1:
                per_tap = conv_filter(act_pad, cube(kept_dy))
                kernel_total = kernel_total + per_tap.transpose(1, 2, 3, 0, 4).reshape(taps * channels, channels)
                if micro == micro_count - 1:
                    kernel_term = (kernel_total * norm_scale).astype(jnp.bfloat16)
                    kernel_term, centre, received, both_pad = lax.optimization_barrier(
                        (kernel_term, centre, received, both_pad)
                    )
            grad_pad = both_pad[..., channels:] if tick == 0 else assemble(cube(centre), received, table)
            grad_act = conv_data(grad_pad, flipped).reshape(row_count, channels)
            result = finish_grad(values, centre, live_now, grad_act, gain_row)
            kept_grad = jnp.where(active, result, kept_grad)
            if tick < n_pipe - 1:
                down = [(p, p - 1) for p in range(1, n_pipe)]
                centre = lax.ppermute(result, "pipe", down)
                received = exchange(cube(result), ("pipe", "sx", "sy"), (n_pipe, n_x, n_y), 1)
        grads_out.append(kept_grad)
    grad_store = jnp.stack(grads_out)
    over_x = scattered_sum(kernel_term, "sx", shard_rows)
    partner = lax.ppermute(over_x, "sy", [(i, i ^ 1) for i in range(n_y)]) if n_y == 2 else None
    if partner is not None:
        kernel_share = over_x + partner
    else:
        kernel_share = lax.psum(over_x, "sy")
    return (grad_store[None, :, None, None], kernel_share[None])


def solution(mesh):
    return jax.shard_map(
        shards,
        mesh=mesh,
        in_specs=(
            P("pipe", None, "sx", "sy", None, None),
            P(None, "sx", "sy", None, None),
            P(None, "sx", "sy", None, None),
            P(None, "sx", "sy"),
            P("pipe", None),
            P("pipe", "sx", None),
        ),
        out_specs=(P("pipe", None, "sx", "sy", None, None), P("pipe", "sx", None)),
        check_vma=False,
    )
```

```python
import jax
import jax.numpy as jnp
from jax import lax
from jax.sharding import PartitionSpec as P

OFFSETS = (-1, 0, 1)


def source_range(offset):
    if offset < 0:
        return slice(7, 8)
    if offset > 0:
        return slice(0, 1)
    return slice(0, 8)


def activate(values, gain_row):
    floats = values.astype(jnp.float32)
    square = jnp.mean(floats * floats, axis=-1, keepdims=True)
    return jax.nn.silu(floats * lax.rsqrt(square + 1e-06) * gain_row)


def with_blank(blocks_in):
    return jnp.concatenate([blocks_in, jnp.zeros_like(blocks_in)], axis=0)


def face_piece(cube, shift_x, shift_y):
    return cube[:, source_range(shift_x), source_range(shift_y)]


def directions():
    return [(sx, sy) for sx in OFFSETS for sy in OFFSETS if (sx, sy) != (0, 0)]


def assemble(centre, received, table, split=False):
    slabs_x = []
    for shift_x in OFFSETS:
        rows_y = []
        for shift_y in OFFSETS:
            column = (shift_x + 1) * 3 + (shift_y + 1)
            piece = centre if (shift_x, shift_y) == (0, 0) else received[(shift_x, shift_y)]
            source = with_blank(piece)
            parts_z = []
            for shift_z in OFFSETS:
                direction = column * 3 + shift_z + 1
                if piece.shape[0] == 1:
                    chosen = table[:, direction][:, None, None, None, None] == 0
                    picked = jnp.where(chosen, piece, jnp.zeros_like(piece))
                else:
                    picked = source[table[:, direction]]
                parts_z.append(picked[:, :, :, source_range(shift_z), :])
            rows_y.append(jnp.concatenate(parts_z, axis=3))
        slabs_x.append(jnp.concatenate(rows_y, axis=2))
    if split:
        slabs_x[0], slabs_x[2] = lax.optimization_barrier((slabs_x[0], slabs_x[2]))
    return jnp.concatenate(slabs_x, axis=1)


def exchange(cube, axes, sizes, pipe_step, carry=None, carried=None):
    n_pipe, n_x, n_y = sizes if pipe_step else (pipe_step + 1, *sizes)

    def linear(p, a, b):
        return (p * n_x + a) * n_y + b if pipe_step else a * n_y + b

    def send(piece, moves):
        route = []
        for p in range(pipe_step, n_pipe):
            for a in range(n_x):
                for b in range(n_y):
                    ta, tb = moves(a, b)
                    if 0 <= ta < n_x and 0 <= tb < n_y:
                        route.append((linear(p, a, b), linear(p - pipe_step, ta, tb)))
        return lax.ppermute(piece, axes, route)

    def face_x(shift_x):
        face = face_piece(cube, shift_x, 0)
        if carry is None:
            return send(face, lambda a, b: (a - shift_x, b))
        rows = carry.shape[-1]
        payload = jnp.concatenate([carry, face.reshape(-1, rows)], axis=0)
        got = send(payload, lambda a, b: ((a - shift_x) % n_x, b))
        carried[(-shift_x) % n_x] = got[: carry.shape[0]]
        return got[carry.shape[0] :].reshape(face.shape)

    received = {}
    if n_y == 2:
        place_y = lax.axis_index("sy")
        for shift_x in OFFSETS:
            if shift_x != 0:
                received[(shift_x, 0)] = face_x(shift_x)
            row = lax.dynamic_slice_in_dim(cube[:, source_range(shift_x)], (1 - place_y) * 7, 1, axis=2)
            got = send(row, lambda a, b, i=shift_x: (a - i, 1 - b))
            blank = jnp.zeros_like(got)
            received[(shift_x, 1)] = jnp.where(place_y == 0, got, blank)
            received[(shift_x, -1)] = jnp.where(place_y == 1, got, blank)
        return received
    for shift_x, shift_y in directions():
        if shift_y == 0:
            received[(shift_x, 0)] = face_x(shift_x)
            continue
        received[(shift_x, shift_y)] = send(
            face_piece(cube, shift_x, shift_y), lambda a, b, i=shift_x, j=shift_y: (a - i, b - j)
        )
    return received


def conv_data(padded, filters):
    return lax.conv_general_dilated(
        padded,
        filters,
        (1, 1, 1),
        "VALID",
        dimension_numbers=("NDHWC", "DHWIO", "NDHWC"),
        preferred_element_type=jnp.float32,
    )


def conv_filter(padded, grad_cube):
    return lax.conv_general_dilated(
        padded,
        grad_cube,
        (1, 1, 1),
        "VALID",
        dimension_numbers=("CDHWN", "IDHWO", "NDHWC"),
        preferred_element_type=jnp.float32,
    )


def gathered(shard, axis, given):
    count = lax.axis_size(axis)
    place = lax.axis_index(axis)
    parts = [shard]
    for step in range(1, count):
        if step in given:
            parts.append(given[step])
        else:
            parts.append(lax.ppermute(shard, axis, [(i, (i + step) % count) for i in range(count)]))
    ordered = jnp.stack(parts)
    index = (place - jnp.arange(count)) % count
    slots = jnp.zeros((count,), jnp.int32).at[index].set(jnp.arange(count, dtype=jnp.int32))
    return ordered[slots].reshape(count * shard.shape[0], *shard.shape[1:])


def scattered_sum(full, axis, share_rows):
    count = lax.axis_size(axis)
    place = lax.axis_index(axis)
    total = lax.dynamic_slice_in_dim(full, place * share_rows, share_rows, axis=0).astype(jnp.float32)
    for step in range(1, count):
        target = (place + step) % count
        piece = lax.dynamic_slice_in_dim(full, target * share_rows, share_rows, axis=0)
        total = total + lax.ppermute(piece, axis, [(i, (i + step) % count) for i in range(count)]).astype(
            jnp.float32
        )
    return total


def reduced_rows(term, share_rows):
    over_x = scattered_sum(term, "sx", share_rows)
    if lax.axis_size("sy") == 2:
        return over_x + lax.ppermute(over_x, "sy", [(0, 1), (1, 0)])
    return lax.psum(over_x, "sy")


def finish_grad(values, grad_live, live_now, grad_act, gain_row):
    _, pullback = jax.vjp(lambda floats: activate(floats, gain_row), values.astype(jnp.float32))
    (through,) = pullback(grad_act)
    summed = grad_live.astype(jnp.float32) + through
    result = jnp.where(live_now[:, None], summed, jnp.zeros_like(summed))
    return result.astype(jnp.bfloat16)


def shards(segment_inputs, out_cotangent, neighbours, block_counts, norm_gain, kernel):
    n_pipe = lax.axis_size("pipe")
    n_x = lax.axis_size("sx")
    n_y = lax.axis_size("sy")
    segment_place = lax.axis_index("pipe")
    micro_count = segment_inputs.shape[1]
    row_count = segment_inputs.shape[4]
    channels = segment_inputs.shape[5]
    blocks = row_count // 512
    taps = 27
    gain_row = norm_gain[0]
    inputs = segment_inputs[0, :, 0, 0]
    cotangent = out_cotangent[:, 0, 0]
    tables = neighbours[:, 0, 0]
    slot_ids = jnp.arange(row_count, dtype=jnp.int32) // 512
    live_rows = slot_ids[None, :] < block_counts[:, 0, 0][:, None]

    def cube(values):
        return values.reshape(blocks, 8, 8, 8, channels)

    grads_out = []
    kernel_total = jnp.zeros((taps * channels, channels), jnp.float32)
    norm_scale = float(n_x * n_y * micro_count * row_count) ** (-0.5)
    shard_rows = kernel.shape[1]
    kernel_term = None
    kernel_share = None
    shifted = micro_count == 1 and n_pipe >= 2
    for micro in range(micro_count):
        table = tables[micro]
        live_now = live_rows[micro]
        values = inputs[micro]
        activation = activate(values, gain_row).astype(jnp.bfloat16)
        start = cotangent[micro]
        start = jnp.where(live_now[:, None], start, jnp.zeros_like(start))
        both = jnp.concatenate([cube(activation), cube(start)], axis=-1)
        if micro == 0:
            carried = {}
            riding = kernel[0] if n_x >= 3 else None
            got = exchange(both, ("sx", "sy"), (n_x, n_y), 0, riding, carried)
            weights = gathered(kernel[0], "sx", carried)
            flipped = weights.reshape(3, 3, 3, channels, channels)[::-1, ::-1, ::-1].transpose(0, 1, 2, 4, 3)
        else:
            got = exchange(both, ("sx", "sy"), (n_x, n_y), 0)
        both_pad = assemble(both, got, table, split=True)
        act_pad = both_pad[..., :channels]
        if shifted:
            act_up = lax.ppermute(act_pad, "pipe", [(q, (q + 1) % n_pipe) for q in range(n_pipe)])
        centre = start
        received = None
        kept_dy = start
        kept_grad = jnp.zeros((row_count, channels), jnp.bfloat16)
        for tick in range(n_pipe):
            active = segment_place == n_pipe - 1 - tick
            kept_dy = jnp.where(active, centre, kept_dy)
            if tick == n_pipe - 1 and not shifted:
                per_tap = conv_filter(act_pad, cube(kept_dy))
                kernel_total = kernel_total + per_tap.transpose(1, 2, 3, 0, 4).reshape(taps * channels, channels)
                if micro == micro_count - 1:
                    kernel_term = (kernel_total * norm_scale).astype(jnp.bfloat16)
                    kernel_term, centre, received, both_pad = lax.optimization_barrier(
                        (kernel_term, centre, received, both_pad)
                    )
            grad_pad = both_pad[..., channels:] if tick == 0 else assemble(cube(centre), received, table)
            grad_act = conv_data(grad_pad, flipped).reshape(row_count, channels)
            result = finish_grad(values, centre, live_now, grad_act, gain_row)
            kept_grad = jnp.where(active, result, kept_grad)
            if shifted and tick == n_pipe - 2:
                up_dy = jnp.where(segment_place == 0, start, kept_grad)
                per_tap = conv_filter(act_up, cube(up_dy))
                term = per_tap.transpose(1, 2, 3, 0, 4).reshape(taps * channels, channels) * norm_scale
                share_up = reduced_rows(term.astype(jnp.bfloat16), shard_rows)
                kernel_share = lax.ppermute(share_up, "pipe", [(q, (q - 1) % n_pipe) for q in range(n_pipe)])
            if tick < n_pipe - 1:
                down = [(p, p - 1) for p in range(1, n_pipe)]
                centre = lax.ppermute(result, "pipe", down)
                received = exchange(cube(result), ("pipe", "sx", "sy"), (n_pipe, n_x, n_y), 1)
        grads_out.append(kept_grad)
    grad_store = jnp.stack(grads_out)
    if not shifted:
        kernel_share = reduced_rows(kernel_term, shard_rows)
    return (grad_store[None, :, None, None], kernel_share[None])


def solution(mesh):
    return jax.shard_map(
        shards,
        mesh=mesh,
        in_specs=(
            P("pipe", None, "sx", "sy", None, None),
            P(None, "sx", "sy", None, None),
            P(None, "sx", "sy", None, None),
            P(None, "sx", "sy"),
            P("pipe", None),
            P("pipe", "sx", None),
        ),
        out_specs=(P("pipe", None, "sx", "sy", None, None), P("pipe", "sx", None)),
        check_vma=False,
    )
```

```python
import jax
import jax.numpy as jnp
from jax import lax
from jax.sharding import PartitionSpec as P

OFFSETS = (-1, 0, 1)


def source_range(offset):
    if offset < 0:
        return slice(7, 8)
    if offset > 0:
        return slice(0, 1)
    return slice(0, 8)


def activate(values, gain_row):
    floats = values.astype(jnp.float32)
    square = jnp.mean(floats * floats, axis=-1, keepdims=True)
    return jax.nn.silu(floats * lax.rsqrt(square + 1e-06) * gain_row)


def with_blank(blocks_in):
    return jnp.concatenate([blocks_in, jnp.zeros_like(blocks_in)], axis=0)


def face_piece(cube, shift_x, shift_y):
    return cube[:, source_range(shift_x), source_range(shift_y)]


def directions():
    return [(sx, sy) for sx in OFFSETS for sy in OFFSETS if (sx, sy) != (0, 0)]


def assemble(centre, received, table, split=False):
    slabs_x = []
    for shift_x in OFFSETS:
        rows_y = []
        for shift_y in OFFSETS:
            column = (shift_x + 1) * 3 + (shift_y + 1)
            piece = centre if (shift_x, shift_y) == (0, 0) else received[(shift_x, shift_y)]
            source = with_blank(piece)
            parts_z = []
            for shift_z in OFFSETS:
                direction = column * 3 + shift_z + 1
                if piece.shape[0] == 1:
                    chosen = table[:, direction][:, None, None, None, None] == 0
                    picked = jnp.where(chosen, piece, jnp.zeros_like(piece))
                else:
                    picked = source[table[:, direction]]
                parts_z.append(picked[:, :, :, source_range(shift_z), :])
            rows_y.append(jnp.concatenate(parts_z, axis=3))
        slabs_x.append(jnp.concatenate(rows_y, axis=2))
    if split:
        slabs_x[0], slabs_x[2] = lax.optimization_barrier((slabs_x[0], slabs_x[2]))
    return jnp.concatenate(slabs_x, axis=1)


def exchange(cube, axes, sizes, pipe_step, carry=None, carried=None):
    n_pipe, n_x, n_y = sizes if pipe_step else (pipe_step + 1, *sizes)

    def linear(p, a, b):
        return (p * n_x + a) * n_y + b if pipe_step else a * n_y + b

    def send(piece, moves):
        route = []
        for p in range(pipe_step, n_pipe):
            for a in range(n_x):
                for b in range(n_y):
                    ta, tb = moves(a, b)
                    if 0 <= ta < n_x and 0 <= tb < n_y:
                        route.append((linear(p, a, b), linear(p - pipe_step, ta, tb)))
        return lax.ppermute(piece, axes, route)

    def face_x(shift_x):
        face = face_piece(cube, shift_x, 0)
        if carry is None:
            return send(face, lambda a, b: (a - shift_x, b))
        rows = carry.shape[-1]
        payload = jnp.concatenate([carry, face.reshape(-1, rows)], axis=0)
        got = send(payload, lambda a, b: ((a - shift_x) % n_x, b))
        carried[(-shift_x) % n_x] = got[: carry.shape[0]]
        return got[carry.shape[0] :].reshape(face.shape)

    received = {}
    if n_y == 2:
        place_y = lax.axis_index("sy")
        for shift_x in OFFSETS:
            if shift_x != 0:
                received[(shift_x, 0)] = face_x(shift_x)
            row = lax.dynamic_slice_in_dim(cube[:, source_range(shift_x)], (1 - place_y) * 7, 1, axis=2)
            got = send(row, lambda a, b, i=shift_x: (a - i, 1 - b))
            blank = jnp.zeros_like(got)
            received[(shift_x, 1)] = jnp.where(place_y == 0, got, blank)
            received[(shift_x, -1)] = jnp.where(place_y == 1, got, blank)
        return received
    for shift_x, shift_y in directions():
        if shift_y == 0:
            received[(shift_x, 0)] = face_x(shift_x)
            continue
        received[(shift_x, shift_y)] = send(
            face_piece(cube, shift_x, shift_y), lambda a, b, i=shift_x, j=shift_y: (a - i, b - j)
        )
    return received


def conv_data(padded, filters):
    return lax.conv_general_dilated(
        padded,
        filters,
        (1, 1, 1),
        "VALID",
        dimension_numbers=("NDHWC", "DHWOI", "NDHWC"),
        preferred_element_type=jnp.float32,
    )


def conv_filter(padded, grad_cube):
    return lax.conv_general_dilated(
        padded,
        grad_cube,
        (1, 1, 1),
        "VALID",
        dimension_numbers=("CDHWN", "IDHWO", "NDHWC"),
        preferred_element_type=jnp.float32,
    )


def gathered(shard, axis, given):
    count = lax.axis_size(axis)
    place = lax.axis_index(axis)
    parts = [shard]
    for step in range(1, count):
        if step in given:
            parts.append(given[step])
        else:
            parts.append(lax.ppermute(shard, axis, [(i, (i + step) % count) for i in range(count)]))
    backwards = jnp.stack(parts[::-1] * 2)
    ordered = lax.dynamic_slice_in_dim(backwards, count - 1 - place, count, axis=0)
    return ordered.reshape(count * shard.shape[0], *shard.shape[1:])


def scattered_sum(full, axis, share_rows):
    count = lax.axis_size(axis)
    place = lax.axis_index(axis)
    total = lax.dynamic_slice_in_dim(full, place * share_rows, share_rows, axis=0).astype(jnp.float32)
    for step in range(1, count):
        target = (place + step) % count
        piece = lax.dynamic_slice_in_dim(full, target * share_rows, share_rows, axis=0)
        total = total + lax.ppermute(piece, axis, [(i, (i + step) % count) for i in range(count)]).astype(
            jnp.float32
        )
    return total


def finish_grad(values, grad_live, live_now, grad_act, gain_row):
    _, pullback = jax.vjp(lambda floats: activate(floats, gain_row), values.astype(jnp.float32))
    (through,) = pullback(grad_act)
    summed = grad_live.astype(jnp.float32) + through
    result = jnp.where(live_now[:, None], summed, jnp.zeros_like(summed))
    return result.astype(jnp.bfloat16)


def shards(segment_inputs, out_cotangent, neighbours, block_counts, norm_gain, kernel):
    n_pipe = lax.axis_size("pipe")
    n_x = lax.axis_size("sx")
    n_y = lax.axis_size("sy")
    segment_place = lax.axis_index("pipe")
    micro_count = segment_inputs.shape[1]
    row_count = segment_inputs.shape[4]
    channels = segment_inputs.shape[5]
    blocks = row_count // 512
    taps = 27
    gain_row = norm_gain[0]
    inputs = segment_inputs[0, :, 0, 0]
    cotangent = out_cotangent[:, 0, 0]
    tables = neighbours[:, 0, 0]
    slot_ids = jnp.arange(row_count, dtype=jnp.int32) // 512
    live_rows = slot_ids[None, :] < block_counts[:, 0, 0][:, None]

    def cube(values):
        return values.reshape(blocks, 8, 8, 8, channels)

    grads_out = []
    kernel_total = jnp.zeros((taps * channels, channels), jnp.float32)
    norm_scale = float(n_x * n_y * micro_count * row_count) ** (-0.5)
    shard_rows = kernel.shape[1]
    kernel_term = None
    for micro in range(micro_count):
        table = tables[micro]
        live_now = live_rows[micro]
        values = inputs[micro]
        activation = activate(values, gain_row).astype(jnp.bfloat16)
        start = cotangent[micro]
        start = jnp.where(live_now[:, None], start, jnp.zeros_like(start))
        both = jnp.concatenate([cube(activation), cube(start)], axis=-1)
        if micro == 0:
            carried = {}
            riding = kernel[0] if n_x >= 3 else None
            got = exchange(both, ("sx", "sy"), (n_x, n_y), 0, riding, carried)
            weights = gathered(kernel[0], "sx", carried)
            flipped = weights.reshape(3, 3, 3, channels, channels)[::-1, ::-1, ::-1]
        else:
            got = exchange(both, ("sx", "sy"), (n_x, n_y), 0)
        both_pad = assemble(both, got, table, split=True)
        act_pad = both_pad[..., :channels]
        centre = start
        received = None
        kept_dy = start
        kept_grad = jnp.zeros((row_count, channels), jnp.bfloat16)
        for tick in range(n_pipe):
            active = segment_place == n_pipe - 1 - tick
            kept_dy = jnp.where(active, centre, kept_dy)
            if tick == n_pipe - 1:
                per_tap = conv_filter(act_pad, cube(kept_dy))
                kernel_total = kernel_total + per_tap.transpose(1, 2, 3, 0, 4).reshape(taps * channels, channels)
                if micro == micro_count - 1:
                    kernel_term = (kernel_total * norm_scale).astype(jnp.bfloat16)
                    kernel_term, centre, received, both_pad = lax.optimization_barrier(
                        (kernel_term, centre, received, both_pad)
                    )
            grad_pad = both_pad[..., channels:] if tick == 0 else assemble(cube(centre), received, table)
            grad_act = conv_data(grad_pad, flipped).reshape(row_count, channels)
            result = finish_grad(values, centre, live_now, grad_act, gain_row)
            kept_grad = jnp.where(active, result, kept_grad)
            if tick < n_pipe - 1:
                down = [(p, p - 1) for p in range(1, n_pipe)]
                centre = lax.ppermute(result, "pipe", down)
                received = exchange(cube(result), ("pipe", "sx", "sy"), (n_pipe, n_x, n_y), 1)
        grads_out.append(kept_grad)
    grad_store = jnp.stack(grads_out)
    over_x = scattered_sum(kernel_term, "sx", shard_rows)
    partner = lax.ppermute(over_x, "sy", [(i, i ^ 1) for i in range(n_y)]) if n_y == 2 else None
    if partner is not None:
        kernel_share = over_x + partner
    else:
        kernel_share = lax.psum(over_x, "sy")
    return (grad_store[None, :, None, None], kernel_share[None])


def solution(mesh):
    return jax.shard_map(
        shards,
        mesh=mesh,
        in_specs=(
            P("pipe", None, "sx", "sy", None, None),
            P(None, "sx", "sy", None, None),
            P(None, "sx", "sy", None, None),
            P(None, "sx", "sy"),
            P("pipe", None),
            P("pipe", "sx", None),
        ),
        out_specs=(P("pipe", None, "sx", "sy", None, None), P("pipe", "sx", None)),
        check_vma=False,
    )
```

```python
import jax
import jax.numpy as jnp
from jax import lax
from jax.sharding import PartitionSpec as P

OFFSETS = (-1, 0, 1)


def source_range(offset):
    if offset < 0:
        return slice(7, 8)
    if offset > 0:
        return slice(0, 1)
    return slice(0, 8)


def activate(values, gain_row):
    floats = values.astype(jnp.float32)
    square = jnp.mean(floats * floats, axis=-1, keepdims=True)
    return jax.nn.silu(floats * lax.rsqrt(square + 1e-06) * gain_row)


def with_blank(blocks_in):
    return jnp.concatenate([blocks_in, jnp.zeros_like(blocks_in)], axis=0)


def face_piece(cube, shift_x, shift_y):
    return cube[:, source_range(shift_x), source_range(shift_y)]


def directions():
    return [(sx, sy) for sx in OFFSETS for sy in OFFSETS if (sx, sy) != (0, 0)]


def assemble(centre, received, table, split=False):
    slabs_x = []
    for shift_x in OFFSETS:
        rows_y = []
        for shift_y in OFFSETS:
            column = (shift_x + 1) * 3 + (shift_y + 1)
            piece = centre if (shift_x, shift_y) == (0, 0) else received[(shift_x, shift_y)]
            source = with_blank(piece)
            parts_z = []
            for shift_z in OFFSETS:
                direction = column * 3 + shift_z + 1
                if piece.shape[0] == 1:
                    chosen = table[:, direction][:, None, None, None, None] == 0
                    picked = jnp.where(chosen, piece, jnp.zeros_like(piece))
                else:
                    picked = source[table[:, direction]]
                parts_z.append(picked[:, :, :, source_range(shift_z), :])
            rows_y.append(jnp.concatenate(parts_z, axis=3))
        slabs_x.append(jnp.concatenate(rows_y, axis=2))
    if split:
        slabs_x[0], slabs_x[2] = lax.optimization_barrier((slabs_x[0], slabs_x[2]))
    return jnp.concatenate(slabs_x, axis=1)


def exchange(cube, axes, sizes, pipe_step, carry=None, carried=None):
    n_pipe, n_x, n_y = sizes if pipe_step else (pipe_step + 1, *sizes)

    def linear(p, a, b):
        return (p * n_x + a) * n_y + b if pipe_step else a * n_y + b

    def send(piece, moves):
        route = []
        for p in range(pipe_step, n_pipe):
            for a in range(n_x):
                for b in range(n_y):
                    ta, tb = moves(a, b)
                    if 0 <= ta < n_x and 0 <= tb < n_y:
                        route.append((linear(p, a, b), linear(p - pipe_step, ta, tb)))
        return lax.ppermute(piece, axes, route)

    def face_x(shift_x):
        face = face_piece(cube, shift_x, 0)
        if carry is None:
            return send(face, lambda a, b: (a - shift_x, b))
        rows = carry.shape[-1]
        payload = jnp.concatenate([carry, face.reshape(-1, rows)], axis=0)
        got = send(payload, lambda a, b: ((a - shift_x) % n_x, b))
        carried[(-shift_x) % n_x] = got[: carry.shape[0]]
        return got[carry.shape[0] :].reshape(face.shape)

    received = {}
    if n_y == 2:
        place_y = lax.axis_index("sy")
        for shift_x in OFFSETS:
            if shift_x != 0:
                received[(shift_x, 0)] = face_x(shift_x)
            row = lax.dynamic_slice_in_dim(cube[:, source_range(shift_x)], (1 - place_y) * 7, 1, axis=2)
            got = send(row, lambda a, b, i=shift_x: (a - i, 1 - b))
            blank = jnp.zeros_like(got)
            received[(shift_x, 1)] = jnp.where(place_y == 0, got, blank)
            received[(shift_x, -1)] = jnp.where(place_y == 1, got, blank)
        return received
    for shift_x, shift_y in directions():
        if shift_y == 0:
            received[(shift_x, 0)] = face_x(shift_x)
            continue
        received[(shift_x, shift_y)] = send(
            face_piece(cube, shift_x, shift_y), lambda a, b, i=shift_x, j=shift_y: (a - i, b - j)
        )
    return received


def conv_data(padded, filters):
    return lax.conv_general_dilated(
        padded,
        filters,
        (1, 1, 1),
        "VALID",
        dimension_numbers=("NDHWC", "DHWIO", "NDHWC"),
        preferred_element_type=jnp.float32,
    )


def conv_filter(padded, grad_cube):
    return lax.conv_general_dilated(
        padded,
        grad_cube,
        (1, 1, 1),
        "VALID",
        dimension_numbers=("CDHWN", "IDHWO", "NDHWC"),
        preferred_element_type=jnp.float32,
    )


def gathered(shard, axis, given):
    count = lax.axis_size(axis)
    place = lax.axis_index(axis)
    parts = [shard]
    for step in range(1, count):
        if step in given:
            parts.append(given[step])
        else:
            parts.append(lax.ppermute(shard, axis, [(i, (i + step) % count) for i in range(count)]))
    ordered = jnp.stack(parts)
    index = (place - jnp.arange(count)) % count
    slots = jnp.zeros((count,), jnp.int32).at[index].set(jnp.arange(count, dtype=jnp.int32))
    return ordered[slots].reshape(count * shard.shape[0], *shard.shape[1:])


def scattered_sum(full, axis, share_rows):
    count = lax.axis_size(axis)
    place = lax.axis_index(axis)
    total = lax.dynamic_slice_in_dim(full, place * share_rows, share_rows, axis=0).astype(jnp.float32)
    for step in range(1, count):
        target = (place + step) % count
        piece = lax.dynamic_slice_in_dim(full, target * share_rows, share_rows, axis=0)
        total = total + lax.ppermute(piece, axis, [(i, (i + step) % count) for i in range(count)]).astype(
            jnp.float32
        )
    return total


def finish_grad(values, grad_live, live_now, grad_act, gain_row):
    _, pullback = jax.vjp(lambda floats: activate(floats, gain_row), values.astype(jnp.float32))
    (through,) = pullback(grad_act)
    summed = grad_live.astype(jnp.float32) + through
    result = jnp.where(live_now[:, None], summed, jnp.zeros_like(summed))
    return result.astype(jnp.bfloat16)


def shards(segment_inputs, out_cotangent, neighbours, block_counts, norm_gain, kernel):
    n_pipe = lax.axis_size("pipe")
    n_x = lax.axis_size("sx")
    n_y = lax.axis_size("sy")
    segment_place = lax.axis_index("pipe")
    micro_count = segment_inputs.shape[1]
    row_count = segment_inputs.shape[4]
    channels = segment_inputs.shape[5]
    blocks = row_count // 512
    taps = 27
    gain_row = norm_gain[0]
    inputs = segment_inputs[0, :, 0, 0]
    cotangent = out_cotangent[:, 0, 0]
    tables = neighbours[:, 0, 0]
    slot_ids = jnp.arange(row_count, dtype=jnp.int32) // 512
    live_rows = slot_ids[None, :] < block_counts[:, 0, 0][:, None]

    def cube(values):
        return values.reshape(blocks, 8, 8, 8, channels)

    grads_out = []
    kernel_total = jnp.zeros((taps * channels, channels), jnp.float32)
    norm_scale = float(n_x * n_y * micro_count * row_count) ** (-0.5)
    shard_rows = kernel.shape[1]
    kernel_term = None
    for micro in range(micro_count):
        table = tables[micro]
        live_now = live_rows[micro]
        values = inputs[micro]
        start = cotangent[micro]
        start = jnp.where(live_now[:, None], start, jnp.zeros_like(start))
        both = jnp.concatenate([cube(values), cube(start)], axis=-1)
        if micro == 0:
            carried = {}
            riding = kernel[0] if n_x >= 3 else None
            got = exchange(both, ("sx", "sy"), (n_x, n_y), 0, riding, carried)
            weights = gathered(kernel[0], "sx", carried)
            flipped = weights.reshape(3, 3, 3, channels, channels)[::-1, ::-1, ::-1].transpose(0, 1, 2, 4, 3)
        else:
            got = exchange(both, ("sx", "sy"), (n_x, n_y), 0)
        both_pad = assemble(both, got, table, split=True)
        act_pad = activate(both_pad[..., :channels], gain_row).astype(jnp.bfloat16)
        centre = start
        received = None
        kept_dy = start
        kept_grad = jnp.zeros((row_count, channels), jnp.bfloat16)
        for tick in range(n_pipe):
            active = segment_place == n_pipe - 1 - tick
            kept_dy = jnp.where(active, centre, kept_dy)
            if tick == n_pipe - 1:
                per_tap = conv_filter(act_pad, cube(kept_dy))
                kernel_total = kernel_total + per_tap.transpose(1, 2, 3, 0, 4).reshape(taps * channels, channels)
                if micro == micro_count - 1:
                    kernel_term = (kernel_total * norm_scale).astype(jnp.bfloat16)
                    kernel_term, centre, received, both_pad = lax.optimization_barrier(
                        (kernel_term, centre, received, both_pad)
                    )
            grad_pad = both_pad[..., channels:] if tick == 0 else assemble(cube(centre), received, table)
            grad_act = conv_data(grad_pad, flipped).reshape(row_count, channels)
            result = finish_grad(values, centre, live_now, grad_act, gain_row)
            kept_grad = jnp.where(active, result, kept_grad)
            if tick < n_pipe - 1:
                down = [(p, p - 1) for p in range(1, n_pipe)]
                centre = lax.ppermute(result, "pipe", down)
                received = exchange(cube(result), ("pipe", "sx", "sy"), (n_pipe, n_x, n_y), 1)
        grads_out.append(kept_grad)
    grad_store = jnp.stack(grads_out)
    over_x = scattered_sum(kernel_term, "sx", shard_rows)
    partner = lax.ppermute(over_x, "sy", [(i, i ^ 1) for i in range(n_y)]) if n_y == 2 else None
    if partner is not None:
        kernel_share = over_x + partner
    else:
        kernel_share = lax.psum(over_x, "sy")
    return (grad_store[None, :, None, None], kernel_share[None])


def solution(mesh):
    return jax.shard_map(
        shards,
        mesh=mesh,
        in_specs=(
            P("pipe", None, "sx", "sy", None, None),
            P(None, "sx", "sy", None, None),
            P(None, "sx", "sy", None, None),
            P(None, "sx", "sy"),
            P("pipe", None),
            P("pipe", "sx", None),
        ),
        out_specs=(P("pipe", None, "sx", "sy", None, None), P("pipe", "sx", None)),
        check_vma=False,
    )
```

```python
import jax
import jax.numpy as jnp
from jax import lax
from jax.sharding import PartitionSpec as P

OFFSETS = (-1, 0, 1)


def source_range(offset):
    if offset < 0:
        return slice(7, 8)
    if offset > 0:
        return slice(0, 1)
    return slice(0, 8)


def activate(values, gain_row):
    floats = values.astype(jnp.float32)
    square = jnp.mean(floats * floats, axis=-1, keepdims=True)
    return jax.nn.silu(floats * lax.rsqrt(square + 1e-06) * gain_row)


def with_blank(blocks_in):
    return jnp.concatenate([blocks_in, jnp.zeros_like(blocks_in)], axis=0)


def face_piece(cube, shift_x, shift_y):
    return cube[:, source_range(shift_x), source_range(shift_y)]


def directions():
    return [(sx, sy) for sx in OFFSETS for sy in OFFSETS if (sx, sy) != (0, 0)]


def assemble(centre, received, table, split=False):
    slabs_x = []
    for shift_x in OFFSETS:
        rows_y = []
        for shift_y in OFFSETS:
            column = (shift_x + 1) * 3 + (shift_y + 1)
            piece = centre if (shift_x, shift_y) == (0, 0) else received[(shift_x, shift_y)]
            source = with_blank(piece)
            parts_z = []
            for shift_z in OFFSETS:
                direction = column * 3 + shift_z + 1
                if piece.shape[0] == 1:
                    chosen = table[:, direction][:, None, None, None, None] == 0
                    picked = jnp.where(chosen, piece, jnp.zeros_like(piece))
                else:
                    picked = source[table[:, direction]]
                parts_z.append(picked[:, :, :, source_range(shift_z), :])
            rows_y.append(jnp.concatenate(parts_z, axis=3))
        slabs_x.append(jnp.concatenate(rows_y, axis=2))
    if split:
        slabs_x[0], slabs_x[2] = lax.optimization_barrier((slabs_x[0], slabs_x[2]))
    return jnp.concatenate(slabs_x, axis=1)


def exchange(cube, axes, sizes, pipe_step, carry=None, carried=None):
    n_pipe, n_x, n_y = sizes if pipe_step else (pipe_step + 1, *sizes)

    def linear(p, a, b):
        return (p * n_x + a) * n_y + b if pipe_step else a * n_y + b

    def send(piece, moves):
        route = []
        for p in range(pipe_step, n_pipe):
            for a in range(n_x):
                for b in range(n_y):
                    ta, tb = moves(a, b)
                    if 0 <= ta < n_x and 0 <= tb < n_y:
                        route.append((linear(p, a, b), linear(p - pipe_step, ta, tb)))
        return lax.ppermute(piece, axes, route)

    def face_x(shift_x):
        face = face_piece(cube, shift_x, 0)
        if carry is None:
            return send(face, lambda a, b: (a - shift_x, b))
        rows = carry.shape[-1]
        payload = jnp.concatenate([carry, face.reshape(-1, rows)], axis=0)
        got = send(payload, lambda a, b: ((a - shift_x) % n_x, b))
        carried[(-shift_x) % n_x] = got[: carry.shape[0]]
        return got[carry.shape[0] :].reshape(face.shape)

    received = {}
    if n_y == 2:
        place_y = lax.axis_index("sy")
        for shift_x in OFFSETS:
            if shift_x != 0:
                received[(shift_x, 0)] = face_x(shift_x)
            row = lax.dynamic_slice_in_dim(cube[:, source_range(shift_x)], (1 - place_y) * 7, 1, axis=2)
            got = send(row, lambda a, b, i=shift_x: (a - i, 1 - b))
            blank = jnp.zeros_like(got)
            received[(shift_x, 1)] = jnp.where(place_y == 0, got, blank)
            received[(shift_x, -1)] = jnp.where(place_y == 1, got, blank)
        return received
    for shift_x, shift_y in directions():
        if shift_y == 0:
            received[(shift_x, 0)] = face_x(shift_x)
            continue
        received[(shift_x, shift_y)] = send(
            face_piece(cube, shift_x, shift_y), lambda a, b, i=shift_x, j=shift_y: (a - i, b - j)
        )
    return received


def conv_data(padded, filters):
    return lax.conv_general_dilated(
        padded,
        filters,
        (1, 1, 1),
        "VALID",
        dimension_numbers=("NDHWC", "DHWIO", "NDHWC"),
        preferred_element_type=jnp.float32,
    )


def conv_filter(padded, grad_cube):
    return lax.conv_general_dilated(
        padded,
        grad_cube,
        (1, 1, 1),
        "VALID",
        dimension_numbers=("CDHWN", "IDHWO", "NDHWC"),
        preferred_element_type=jnp.float32,
    )


def gathered(shard, axis, given):
    count = lax.axis_size(axis)
    place = lax.axis_index(axis)
    parts = [shard]
    for step in range(1, count):
        if step in given:
            parts.append(given[step])
        else:
            parts.append(lax.ppermute(shard, axis, [(i, (i + step) % count) for i in range(count)]))
    ordered = jnp.stack(parts)
    index = (place - jnp.arange(count)) % count
    slots = jnp.zeros((count,), jnp.int32).at[index].set(jnp.arange(count, dtype=jnp.int32))
    return ordered[slots].reshape(count * shard.shape[0], *shard.shape[1:])


def scattered_sum(full, axis, share_rows):
    count = lax.axis_size(axis)
    place = lax.axis_index(axis)
    total = lax.dynamic_slice_in_dim(full, place * share_rows, share_rows, axis=0).astype(jnp.float32)
    for step in range(1, count):
        target = (place + step) % count
        piece = lax.dynamic_slice_in_dim(full, target * share_rows, share_rows, axis=0)
        total = total + lax.ppermute(piece, axis, [(i, (i + step) % count) for i in range(count)]).astype(
            jnp.float32
        )
    return total


def finish_grad(values, grad_live, live_now, grad_act, gain_row):
    _, pullback = jax.vjp(lambda floats: activate(floats, gain_row), values.astype(jnp.float32))
    (through,) = pullback(grad_act)
    summed = grad_live.astype(jnp.float32) + through
    result = jnp.where(live_now[:, None], summed, jnp.zeros_like(summed))
    return result.astype(jnp.bfloat16)


def shards(segment_inputs, out_cotangent, neighbours, block_counts, norm_gain, kernel):
    n_pipe = lax.axis_size("pipe")
    n_x = lax.axis_size("sx")
    n_y = lax.axis_size("sy")
    segment_place = lax.axis_index("pipe")
    micro_count = segment_inputs.shape[1]
    row_count = segment_inputs.shape[4]
    channels = segment_inputs.shape[5]
    blocks = row_count // 512
    taps = 27
    gain_row = norm_gain[0]
    inputs = segment_inputs[0, :, 0, 0]
    cotangent = out_cotangent[:, 0, 0]
    tables = neighbours[:, 0, 0]
    slot_ids = jnp.arange(row_count, dtype=jnp.int32) // 512
    live_rows = slot_ids[None, :] < block_counts[:, 0, 0][:, None]

    def cube(values):
        return values.reshape(blocks, 8, 8, 8, channels)

    grads_out = []
    kernel_total = jnp.zeros((taps * channels, channels), jnp.float32)
    norm_scale = float(n_x * n_y * micro_count * row_count) ** (-0.5)
    shard_rows = kernel.shape[1]
    kernel_term = None
    for micro in range(micro_count):
        table = tables[micro]
        live_now = live_rows[micro]
        values = inputs[micro]
        activation = activate(values, gain_row).astype(jnp.bfloat16)
        start = cotangent[micro]
        start = jnp.where(live_now[:, None], start, jnp.zeros_like(start))
        both = jnp.concatenate([cube(activation), cube(start)], axis=-1)
        if micro == 0:
            carried = {}
            riding = kernel[0] if n_x >= 3 else None
            got = exchange(both, ("sx", "sy"), (n_x, n_y), 0, riding, carried)
            weights = gathered(kernel[0], "sx", carried)
            flipped = weights.reshape(3, 3, 3, channels, channels)[::-1, ::-1, ::-1].transpose(0, 1, 2, 4, 3)
        else:
            got = exchange(both, ("sx", "sy"), (n_x, n_y), 0)
        both_pad = assemble(both, got, table, split=True)
        act_pad = both_pad[..., :channels]
        centre = start
        received = None
        kept_dy = start
        kept_grad = jnp.zeros((row_count, channels), jnp.bfloat16)
        keys = directions()
        down = [(p, p - 1) for p in range(1, n_pipe)]

        def middle(tick, carry):
            centre, pieces, kept_dy, kept_grad = carry
            active = segment_place == n_pipe - 1 - tick
            kept_dy = jnp.where(active, centre, kept_dy)
            grad_pad = assemble(cube(centre), dict(zip(keys, pieces)), table)
            grad_act = conv_data(grad_pad, flipped).reshape(row_count, channels)
            result = finish_grad(values, centre, live_now, grad_act, gain_row)
            kept_grad = jnp.where(active, result, kept_grad)
            sent = exchange(cube(result), ("pipe", "sx", "sy"), (n_pipe, n_x, n_y), 1)
            return (lax.ppermute(result, "pipe", down), tuple(sent[k] for k in keys), kept_dy, kept_grad)

        for tick in range(n_pipe):
            active = segment_place == n_pipe - 1 - tick
            if 0 < tick < n_pipe - 1:
                if tick == 1:
                    carry = (centre, tuple(received[k] for k in keys), kept_dy, kept_grad)
                    carry = lax.fori_loop(1, n_pipe - 1, middle, carry)
                    centre, pieces, kept_dy, kept_grad = carry
                    received = dict(zip(keys, pieces))
                continue
            kept_dy = jnp.where(active, centre, kept_dy)
            if tick == n_pipe - 1:
                per_tap = conv_filter(act_pad, cube(kept_dy))
                kernel_total = kernel_total + per_tap.transpose(1, 2, 3, 0, 4).reshape(taps * channels, channels)
                if micro == micro_count - 1:
                    kernel_term = (kernel_total * norm_scale).astype(jnp.bfloat16)
                    kernel_term, centre, received, both_pad = lax.optimization_barrier(
                        (kernel_term, centre, received, both_pad)
                    )
            grad_pad = both_pad[..., channels:] if tick == 0 else assemble(cube(centre), received, table)
            grad_act = conv_data(grad_pad, flipped).reshape(row_count, channels)
            result = finish_grad(values, centre, live_now, grad_act, gain_row)
            kept_grad = jnp.where(active, result, kept_grad)
            if tick < n_pipe - 1:
                centre = lax.ppermute(result, "pipe", down)
                received = exchange(cube(result), ("pipe", "sx", "sy"), (n_pipe, n_x, n_y), 1)
        grads_out.append(kept_grad)
    grad_store = jnp.stack(grads_out)
    over_x = scattered_sum(kernel_term, "sx", shard_rows)
    partner = lax.ppermute(over_x, "sy", [(i, i ^ 1) for i in range(n_y)]) if n_y == 2 else None
    if partner is not None:
        kernel_share = over_x + partner
    else:
        kernel_share = lax.psum(over_x, "sy")
    return (grad_store[None, :, None, None], kernel_share[None])


def solution(mesh):
    return jax.shard_map(
        shards,
        mesh=mesh,
        in_specs=(
            P("pipe", None, "sx", "sy", None, None),
            P(None, "sx", "sy", None, None),
            P(None, "sx", "sy", None, None),
            P(None, "sx", "sy"),
            P("pipe", None),
            P("pipe", "sx", None),
        ),
        out_specs=(P("pipe", None, "sx", "sy", None, None), P("pipe", "sx", None)),
        check_vma=False,
    )
```

```python
import jax
import jax.numpy as jnp
from jax import lax
from jax.sharding import PartitionSpec as P

OFFSETS = (-1, 0, 1)


def source_range(offset):
    if offset < 0:
        return slice(7, 8)
    if offset > 0:
        return slice(0, 1)
    return slice(0, 8)


def activate(values, gain_row):
    floats = values.astype(jnp.float32)
    square = jnp.mean(floats * floats, axis=-1, keepdims=True)
    return jax.nn.silu(floats * lax.rsqrt(square + 1e-06) * gain_row)


def with_blank(blocks_in):
    return jnp.concatenate([blocks_in, jnp.zeros_like(blocks_in)], axis=0)


def face_piece(cube, shift_x, shift_y):
    return cube[:, source_range(shift_x), source_range(shift_y)]


def directions():
    return [(sx, sy) for sx in OFFSETS for sy in OFFSETS if (sx, sy) != (0, 0)]


def assemble(centre, received, table, split=False):
    slabs_x = []
    for shift_x in OFFSETS:
        rows_y = []
        for shift_y in OFFSETS:
            column = (shift_x + 1) * 3 + (shift_y + 1)
            piece = centre if (shift_x, shift_y) == (0, 0) else received[(shift_x, shift_y)]
            source = with_blank(piece)
            parts_z = []
            for shift_z in OFFSETS:
                direction = column * 3 + shift_z + 1
                if piece.shape[0] == 1:
                    chosen = table[:, direction][:, None, None, None, None] == 0
                    picked = jnp.where(chosen, piece, jnp.zeros_like(piece))
                else:
                    picked = source[table[:, direction]]
                parts_z.append(picked[:, :, :, source_range(shift_z), :])
            rows_y.append(jnp.concatenate(parts_z, axis=3))
        slabs_x.append(jnp.concatenate(rows_y, axis=2))
    if split:
        slabs_x = list(lax.optimization_barrier(tuple(slabs_x)))
    return jnp.concatenate(slabs_x, axis=1)


def exchange(cube, axes, sizes, pipe_step, carry=None, carried=None):
    n_pipe, n_x, n_y = sizes if pipe_step else (pipe_step + 1, *sizes)

    def linear(p, a, b):
        return (p * n_x + a) * n_y + b if pipe_step else a * n_y + b

    def send(piece, moves):
        route = []
        for p in range(pipe_step, n_pipe):
            for a in range(n_x):
                for b in range(n_y):
                    ta, tb = moves(a, b)
                    if 0 <= ta < n_x and 0 <= tb < n_y:
                        route.append((linear(p, a, b), linear(p - pipe_step, ta, tb)))
        return lax.ppermute(piece, axes, route)

    def face_x(shift_x):
        face = face_piece(cube, shift_x, 0)
        if carry is None:
            return send(face, lambda a, b: (a - shift_x, b))
        rows = carry.shape[-1]
        payload = jnp.concatenate([carry, face.reshape(-1, rows)], axis=0)
        got = send(payload, lambda a, b: ((a - shift_x) % n_x, b))
        carried[(-shift_x) % n_x] = got[: carry.shape[0]]
        return got[carry.shape[0] :].reshape(face.shape)

    received = {}
    if n_y == 2:
        place_y = lax.axis_index("sy")
        for shift_x in OFFSETS:
            if shift_x != 0:
                received[(shift_x, 0)] = face_x(shift_x)
            row = lax.dynamic_slice_in_dim(cube[:, source_range(shift_x)], (1 - place_y) * 7, 1, axis=2)
            got = send(row, lambda a, b, i=shift_x: (a - i, 1 - b))
            blank = jnp.zeros_like(got)
            received[(shift_x, 1)] = jnp.where(place_y == 0, got, blank)
            received[(shift_x, -1)] = jnp.where(place_y == 1, got, blank)
        return received
    for shift_x, shift_y in directions():
        if shift_y == 0:
            received[(shift_x, 0)] = face_x(shift_x)
            continue
        received[(shift_x, shift_y)] = send(
            face_piece(cube, shift_x, shift_y), lambda a, b, i=shift_x, j=shift_y: (a - i, b - j)
        )
    return received


def conv_data(padded, filters):
    return lax.conv_general_dilated(
        padded,
        filters,
        (1, 1, 1),
        "VALID",
        dimension_numbers=("NDHWC", "DHWIO", "NDHWC"),
        preferred_element_type=jnp.float32,
    )


def conv_filter(padded, grad_cube):
    return lax.conv_general_dilated(
        padded,
        grad_cube,
        (1, 1, 1),
        "VALID",
        dimension_numbers=("CDHWN", "IDHWO", "NDHWC"),
        preferred_element_type=jnp.float32,
    )


def gathered(shard, axis, given):
    count = lax.axis_size(axis)
    place = lax.axis_index(axis)
    parts = [shard]
    for step in range(1, count):
        if step in given:
            parts.append(given[step])
        else:
            parts.append(lax.ppermute(shard, axis, [(i, (i + step) % count) for i in range(count)]))
    ordered = jnp.stack(parts)
    index = (place - jnp.arange(count)) % count
    slots = jnp.zeros((count,), jnp.int32).at[index].set(jnp.arange(count, dtype=jnp.int32))
    return ordered[slots].reshape(count * shard.shape[0], *shard.shape[1:])


def scattered_sum(full, axis, share_rows):
    count = lax.axis_size(axis)
    place = lax.axis_index(axis)
    total = lax.dynamic_slice_in_dim(full, place * share_rows, share_rows, axis=0).astype(jnp.float32)
    for step in range(1, count):
        target = (place + step) % count
        piece = lax.dynamic_slice_in_dim(full, target * share_rows, share_rows, axis=0)
        total = total + lax.ppermute(piece, axis, [(i, (i + step) % count) for i in range(count)]).astype(
            jnp.float32
        )
    return total


def finish_grad(values, grad_live, live_now, grad_act, gain_row):
    _, pullback = jax.vjp(lambda floats: activate(floats, gain_row), values.astype(jnp.float32))
    (through,) = pullback(grad_act)
    summed = grad_live.astype(jnp.float32) + through
    result = jnp.where(live_now[:, None], summed, jnp.zeros_like(summed))
    return result.astype(jnp.bfloat16)


def shards(segment_inputs, out_cotangent, neighbours, block_counts, norm_gain, kernel):
    n_pipe = lax.axis_size("pipe")
    n_x = lax.axis_size("sx")
    n_y = lax.axis_size("sy")
    segment_place = lax.axis_index("pipe")
    micro_count = segment_inputs.shape[1]
    row_count = segment_inputs.shape[4]
    channels = segment_inputs.shape[5]
    blocks = row_count // 512
    taps = 27
    gain_row = norm_gain[0]
    inputs = segment_inputs[0, :, 0, 0]
    cotangent = out_cotangent[:, 0, 0]
    tables = neighbours[:, 0, 0]
    slot_ids = jnp.arange(row_count, dtype=jnp.int32) // 512
    live_rows = slot_ids[None, :] < block_counts[:, 0, 0][:, None]

    def cube(values):
        return values.reshape(blocks, 8, 8, 8, channels)

    grads_out = []
    kernel_total = jnp.zeros((taps * channels, channels), jnp.float32)
    norm_scale = float(n_x * n_y * micro_count * row_count) ** (-0.5)
    shard_rows = kernel.shape[1]
    kernel_term = None
    for micro in range(micro_count):
        table = tables[micro]
        live_now = live_rows[micro]
        values = inputs[micro]
        activation = activate(values, gain_row).astype(jnp.bfloat16)
        start = cotangent[micro]
        start = jnp.where(live_now[:, None], start, jnp.zeros_like(start))
        both = jnp.concatenate([cube(activation), cube(start)], axis=-1)
        if micro == 0:
            carried = {}
            riding = kernel[0] if n_x >= 3 else None
            got = exchange(both, ("sx", "sy"), (n_x, n_y), 0, riding, carried)
            weights = gathered(kernel[0], "sx", carried)
            flipped = weights.reshape(3, 3, 3, channels, channels)[::-1, ::-1, ::-1].transpose(0, 1, 2, 4, 3)
        else:
            got = exchange(both, ("sx", "sy"), (n_x, n_y), 0)
        both_pad = assemble(both, got, table, split=True)
        act_pad = both_pad[..., :channels]
        centre = start
        received = None
        kept_dy = start
        kept_grad = jnp.zeros((row_count, channels), jnp.bfloat16)
        for tick in range(n_pipe):
            active = segment_place == n_pipe - 1 - tick
            kept_dy = jnp.where(active, centre, kept_dy)
            if tick == n_pipe - 1:
                per_tap = conv_filter(act_pad, cube(kept_dy))
                kernel_total = kernel_total + per_tap.transpose(1, 2, 3, 0, 4).reshape(taps * channels, channels)
                if micro == micro_count - 1:
                    kernel_term = (kernel_total * norm_scale).astype(jnp.bfloat16)
                    kernel_term, centre, received, both_pad = lax.optimization_barrier(
                        (kernel_term, centre, received, both_pad)
                    )
            grad_pad = both_pad[..., channels:] if tick == 0 else assemble(cube(centre), received, table)
            grad_act = conv_data(grad_pad, flipped).reshape(row_count, channels)
            result = finish_grad(values, centre, live_now, grad_act, gain_row)
            kept_grad = jnp.where(active, result, kept_grad)
            if tick < n_pipe - 1:
                down = [(p, p - 1) for p in range(1, n_pipe)]
                centre = lax.ppermute(result, "pipe", down)
                received = exchange(cube(result), ("pipe", "sx", "sy"), (n_pipe, n_x, n_y), 1)
        grads_out.append(kept_grad)
    grad_store = jnp.stack(grads_out)
    over_x = scattered_sum(kernel_term, "sx", shard_rows)
    partner = lax.ppermute(over_x, "sy", [(i, i ^ 1) for i in range(n_y)]) if n_y == 2 else None
    if partner is not None:
        kernel_share = over_x + partner
    else:
        kernel_share = lax.psum(over_x, "sy")
    return (grad_store[None, :, None, None], kernel_share[None])


def solution(mesh):
    return jax.shard_map(
        shards,
        mesh=mesh,
        in_specs=(
            P("pipe", None, "sx", "sy", None, None),
            P(None, "sx", "sy", None, None),
            P(None, "sx", "sy", None, None),
            P(None, "sx", "sy"),
            P("pipe", None),
            P("pipe", "sx", None),
        ),
        out_specs=(P("pipe", None, "sx", "sy", None, None), P("pipe", "sx", None)),
        check_vma=False,
    )
```

```python
import jax
import jax.numpy as jnp
from jax import lax
from jax.sharding import PartitionSpec as P

OFFSETS = (-1, 0, 1)


def source_range(offset):
    if offset < 0:
        return slice(7, 8)
    if offset > 0:
        return slice(0, 1)
    return slice(0, 8)


def activate(values, gain_row):
    floats = values.astype(jnp.float32)
    square = jnp.mean(floats * floats, axis=-1, keepdims=True)
    return jax.nn.silu(floats * lax.rsqrt(square + 1e-06) * gain_row)


def with_blank(blocks_in):
    return jnp.concatenate([blocks_in, jnp.zeros_like(blocks_in)], axis=0)


def face_piece(cube, shift_x, shift_y):
    return cube[:, source_range(shift_x), source_range(shift_y)]


def directions():
    return [(sx, sy) for sx in OFFSETS for sy in OFFSETS if (sx, sy) != (0, 0)]


def assemble(centre, received, table, split=False):
    slabs_x = []
    for shift_x in OFFSETS:
        rows_y = []
        for shift_y in OFFSETS:
            column = (shift_x + 1) * 3 + (shift_y + 1)
            piece = centre if (shift_x, shift_y) == (0, 0) else received[(shift_x, shift_y)]
            source = with_blank(piece)
            parts_z = []
            for shift_z in OFFSETS:
                direction = column * 3 + shift_z + 1
                if piece.shape[0] == 1:
                    chosen = table[:, direction][:, None, None, None, None] == 0
                    picked = jnp.where(chosen, piece, jnp.zeros_like(piece))
                else:
                    picked = source[table[:, direction]]
                parts_z.append(picked[:, :, :, source_range(shift_z), :])
            rows_y.append(jnp.concatenate(parts_z, axis=3))
        slabs_x.append(jnp.concatenate(rows_y, axis=2))
    if split:
        slabs_x[0], slabs_x[2] = lax.optimization_barrier((slabs_x[0], slabs_x[2]))
    return jnp.concatenate(slabs_x, axis=1)


def exchange(cube, axes, sizes, pipe_step, carry=None, carried=None):
    n_pipe, n_x, n_y = sizes if pipe_step else (pipe_step + 1, *sizes)

    def linear(p, a, b):
        return (p * n_x + a) * n_y + b if pipe_step else a * n_y + b

    def send(piece, moves):
        route = []
        for p in range(pipe_step, n_pipe):
            for a in range(n_x):
                for b in range(n_y):
                    ta, tb = moves(a, b)
                    if 0 <= ta < n_x and 0 <= tb < n_y:
                        route.append((linear(p, a, b), linear(p - pipe_step, ta, tb)))
        return lax.ppermute(piece, axes, route)

    def face_x(shift_x):
        face = face_piece(cube, shift_x, 0)
        if carry is None:
            return send(face, lambda a, b: (a - shift_x, b))
        rows = carry.shape[-1]
        payload = jnp.concatenate([carry, face.reshape(-1, rows)], axis=0)
        got = send(payload, lambda a, b: ((a - shift_x) % n_x, b))
        carried[(-shift_x) % n_x] = got[: carry.shape[0]]
        return got[carry.shape[0] :].reshape(face.shape)

    received = {}
    if n_y == 2:
        place_y = lax.axis_index("sy")
        for shift_x in OFFSETS:
            if shift_x != 0:
                received[(shift_x, 0)] = face_x(shift_x)
            row = lax.dynamic_slice_in_dim(cube[:, source_range(shift_x)], (1 - place_y) * 7, 1, axis=2)
            got = send(row, lambda a, b, i=shift_x: (a - i, 1 - b))
            received[(shift_x, 1)] = got
            received[(shift_x, -1)] = got
        return received
    for shift_x, shift_y in directions():
        if shift_y == 0:
            received[(shift_x, 0)] = face_x(shift_x)
            continue
        received[(shift_x, shift_y)] = send(
            face_piece(cube, shift_x, shift_y), lambda a, b, i=shift_x, j=shift_y: (a - i, b - j)
        )
    return received


def conv_data(padded, filters):
    return lax.conv_general_dilated(
        padded,
        filters,
        (1, 1, 1),
        "VALID",
        dimension_numbers=("NDHWC", "DHWIO", "NDHWC"),
        preferred_element_type=jnp.float32,
    )


def conv_filter(padded, grad_cube):
    return lax.conv_general_dilated(
        padded,
        grad_cube,
        (1, 1, 1),
        "VALID",
        dimension_numbers=("CDHWN", "IDHWO", "NDHWC"),
        preferred_element_type=jnp.float32,
    )


def gathered(shard, axis, given):
    count = lax.axis_size(axis)
    place = lax.axis_index(axis)
    parts = [shard]
    for step in range(1, count):
        if step in given:
            parts.append(given[step])
        else:
            parts.append(lax.ppermute(shard, axis, [(i, (i + step) % count) for i in range(count)]))
    ordered = jnp.stack(parts)
    index = (place - jnp.arange(count)) % count
    slots = jnp.zeros((count,), jnp.int32).at[index].set(jnp.arange(count, dtype=jnp.int32))
    return ordered[slots].reshape(count * shard.shape[0], *shard.shape[1:])


def scattered_sum(full, axis, share_rows):
    count = lax.axis_size(axis)
    place = lax.axis_index(axis)
    total = lax.dynamic_slice_in_dim(full, place * share_rows, share_rows, axis=0).astype(jnp.float32)
    for step in range(1, count):
        target = (place + step) % count
        piece = lax.dynamic_slice_in_dim(full, target * share_rows, share_rows, axis=0)
        total = total + lax.ppermute(piece, axis, [(i, (i + step) % count) for i in range(count)]).astype(
            jnp.float32
        )
    return total


def finish_grad(values, grad_live, live_now, grad_act, gain_row):
    _, pullback = jax.vjp(lambda floats: activate(floats, gain_row), values.astype(jnp.float32))
    (through,) = pullback(grad_act)
    summed = grad_live.astype(jnp.float32) + through
    result = jnp.where(live_now[:, None], summed, jnp.zeros_like(summed))
    return result.astype(jnp.bfloat16)


def shards(segment_inputs, out_cotangent, neighbours, block_counts, norm_gain, kernel):
    n_pipe = lax.axis_size("pipe")
    n_x = lax.axis_size("sx")
    n_y = lax.axis_size("sy")
    segment_place = lax.axis_index("pipe")
    micro_count = segment_inputs.shape[1]
    row_count = segment_inputs.shape[4]
    channels = segment_inputs.shape[5]
    blocks = row_count // 512
    taps = 27
    gain_row = norm_gain[0]
    inputs = segment_inputs[0, :, 0, 0]
    cotangent = out_cotangent[:, 0, 0]
    tables = neighbours[:, 0, 0]
    slot_ids = jnp.arange(row_count, dtype=jnp.int32) // 512
    live_rows = slot_ids[None, :] < block_counts[:, 0, 0][:, None]

    def cube(values):
        return values.reshape(blocks, 8, 8, 8, channels)

    grads_out = []
    kernel_total = jnp.zeros((taps * channels, channels), jnp.float32)
    norm_scale = float(n_x * n_y * micro_count * row_count) ** (-0.5)
    shard_rows = kernel.shape[1]
    kernel_term = None
    for micro in range(micro_count):
        table = tables[micro]
        live_now = live_rows[micro]
        values = inputs[micro]
        activation = activate(values, gain_row).astype(jnp.bfloat16)
        start = cotangent[micro]
        start = jnp.where(live_now[:, None], start, jnp.zeros_like(start))
        both = jnp.concatenate([cube(activation), cube(start)], axis=-1)
        if micro == 0:
            carried = {}
            riding = kernel[0] if n_x >= 3 else None
            got = exchange(both, ("sx", "sy"), (n_x, n_y), 0, riding, carried)
            weights = gathered(kernel[0], "sx", carried)
            flipped = weights.reshape(3, 3, 3, channels, channels)[::-1, ::-1, ::-1].transpose(0, 1, 2, 4, 3)
        else:
            got = exchange(both, ("sx", "sy"), (n_x, n_y), 0)
        both_pad = assemble(both, got, table, split=True)
        act_pad = both_pad[..., :channels]
        centre = start
        received = None
        kept_dy = start
        kept_grad = jnp.zeros((row_count, channels), jnp.bfloat16)
        for tick in range(n_pipe):
            active = segment_place == n_pipe - 1 - tick
            kept_dy = jnp.where(active, centre, kept_dy)
            if tick == n_pipe - 1:
                per_tap = conv_filter(act_pad, cube(kept_dy))
                kernel_total = kernel_total + per_tap.transpose(1, 2, 3, 0, 4).reshape(taps * channels, channels)
                if micro == micro_count - 1:
                    kernel_term = (kernel_total * norm_scale).astype(jnp.bfloat16)
                    kernel_term, centre, received, both_pad = lax.optimization_barrier(
                        (kernel_term, centre, received, both_pad)
                    )
            grad_pad = both_pad[..., channels:] if tick == 0 else assemble(cube(centre), received, table)
            grad_act = conv_data(grad_pad, flipped).reshape(row_count, channels)
            result = finish_grad(values, centre, live_now, grad_act, gain_row)
            kept_grad = jnp.where(active, result, kept_grad)
            if tick < n_pipe - 1:
                down = [(p, p - 1) for p in range(1, n_pipe)]
                centre = lax.ppermute(result, "pipe", down)
                received = exchange(cube(result), ("pipe", "sx", "sy"), (n_pipe, n_x, n_y), 1)
        grads_out.append(kept_grad)
    grad_store = jnp.stack(grads_out)
    over_x = scattered_sum(kernel_term, "sx", shard_rows)
    partner = lax.ppermute(over_x, "sy", [(i, i ^ 1) for i in range(n_y)]) if n_y == 2 else None
    if partner is not None:
        kernel_share = over_x + partner
    else:
        kernel_share = lax.psum(over_x, "sy")
    return (grad_store[None, :, None, None], kernel_share[None])


def solution(mesh):
    return jax.shard_map(
        shards,
        mesh=mesh,
        in_specs=(
            P("pipe", None, "sx", "sy", None, None),
            P(None, "sx", "sy", None, None),
            P(None, "sx", "sy", None, None),
            P(None, "sx", "sy"),
            P("pipe", None),
            P("pipe", "sx", None),
        ),
        out_specs=(P("pipe", None, "sx", "sy", None, None), P("pipe", "sx", None)),
        check_vma=False,
    )
```

```python
import jax
import jax.numpy as jnp
from jax import lax
from jax.sharding import PartitionSpec as P

OFFSETS = (-1, 0, 1)


def source_range(offset):
    if offset < 0:
        return slice(7, 8)
    if offset > 0:
        return slice(0, 1)
    return slice(0, 8)


def activate(values, gain_row):
    floats = values.astype(jnp.float32)
    square = jnp.mean(floats * floats, axis=-1, keepdims=True)
    return jax.nn.silu(floats * lax.rsqrt(square + 1e-06) * gain_row)


def with_blank(blocks_in):
    return jnp.concatenate([blocks_in, jnp.zeros_like(blocks_in)], axis=0)


def face_piece(cube, shift_x, shift_y):
    return cube[:, source_range(shift_x), source_range(shift_y)]


def directions():
    return [(sx, sy) for sx in OFFSETS for sy in OFFSETS if (sx, sy) != (0, 0)]


def assemble(centre, received, table, split=False):
    slabs_x = []
    for shift_x in OFFSETS:
        rows_y = []
        for shift_y in OFFSETS:
            column = (shift_x + 1) * 3 + (shift_y + 1)
            piece = centre if (shift_x, shift_y) == (0, 0) else received[(shift_x, shift_y)]
            source = with_blank(piece)
            parts_z = []
            for shift_z in OFFSETS:
                direction = column * 3 + shift_z + 1
                if piece.shape[0] == 1:
                    chosen = table[:, direction][:, None, None, None, None] == 0
                    picked = jnp.where(chosen, piece, jnp.zeros_like(piece))
                else:
                    picked = source[table[:, direction]]
                parts_z.append(picked[:, :, :, source_range(shift_z), :])
            rows_y.append(jnp.concatenate(parts_z, axis=3))
        slabs_x.append(jnp.concatenate(rows_y, axis=2))
    if split:
        slabs_x[0], slabs_x[2] = lax.optimization_barrier((slabs_x[0], slabs_x[2]))
    return jnp.concatenate(slabs_x, axis=1)


def exchange(cube, axes, sizes, pipe_step, carry=None, carried=None):
    n_pipe, n_x, n_y = sizes if pipe_step else (pipe_step + 1, *sizes)

    def linear(p, a, b):
        return (p * n_x + a) * n_y + b if pipe_step else a * n_y + b

    def send(piece, moves):
        route = []
        for p in range(pipe_step, n_pipe):
            for a in range(n_x):
                for b in range(n_y):
                    ta, tb = moves(a, b)
                    if 0 <= ta < n_x and 0 <= tb < n_y:
                        route.append((linear(p, a, b), linear(p - pipe_step, ta, tb)))
        return lax.ppermute(piece, axes, route)

    def face_x(shift_x):
        face = face_piece(cube, shift_x, 0)
        if carry is None:
            return send(face, lambda a, b: (a - shift_x, b))
        rows = carry.shape[-1]
        payload = jnp.concatenate([carry, face.reshape(-1, rows)], axis=0)
        got = send(payload, lambda a, b: ((a - shift_x) % n_x, b))
        carried[(-shift_x) % n_x] = got[: carry.shape[0]]
        return got[carry.shape[0] :].reshape(face.shape)

    received = {}
    if n_y == 2:
        place_y = lax.axis_index("sy")
        for shift_x in OFFSETS:
            if shift_x != 0:
                received[(shift_x, 0)] = face_x(shift_x)
            plane = cube[:, source_range(shift_x)]
            row = jnp.where(place_y == 0, plane[:, :, 7:8], plane[:, :, 0:1])
            got = send(row, lambda a, b, i=shift_x: (a - i, 1 - b))
            received[(shift_x, 1)] = got
            received[(shift_x, -1)] = got
        return received
    for shift_x, shift_y in directions():
        if shift_y == 0:
            received[(shift_x, 0)] = face_x(shift_x)
            continue
        received[(shift_x, shift_y)] = send(
            face_piece(cube, shift_x, shift_y), lambda a, b, i=shift_x, j=shift_y: (a - i, b - j)
        )
    return received


def conv_data(padded, filters):
    return lax.conv_general_dilated(
        padded,
        filters,
        (1, 1, 1),
        "VALID",
        dimension_numbers=("NDHWC", "DHWIO", "NDHWC"),
        preferred_element_type=jnp.float32,
    )


def conv_filter(padded, grad_cube):
    return lax.conv_general_dilated(
        padded,
        grad_cube,
        (1, 1, 1),
        "VALID",
        dimension_numbers=("CDHWN", "IDHWO", "NDHWC"),
        preferred_element_type=jnp.float32,
    )


def gathered(shard, axis, given):
    count = lax.axis_size(axis)
    place = lax.axis_index(axis)
    parts = [shard]
    for step in range(1, count):
        if step in given:
            parts.append(given[step])
        else:
            parts.append(lax.ppermute(shard, axis, [(i, (i + step) % count) for i in range(count)]))
    ordered = jnp.stack(parts)
    index = (place - jnp.arange(count)) % count
    slots = jnp.zeros((count,), jnp.int32).at[index].set(jnp.arange(count, dtype=jnp.int32))
    return ordered[slots].reshape(count * shard.shape[0], *shard.shape[1:])


def scattered_sum(full, axis, share_rows):
    count = lax.axis_size(axis)
    place = lax.axis_index(axis)
    total = lax.dynamic_slice_in_dim(full, place * share_rows, share_rows, axis=0).astype(jnp.float32)
    for step in range(1, count):
        target = (place + step) % count
        piece = lax.dynamic_slice_in_dim(full, target * share_rows, share_rows, axis=0)
        total = total + lax.ppermute(piece, axis, [(i, (i + step) % count) for i in range(count)]).astype(
            jnp.float32
        )
    return total


def finish_grad(values, grad_live, live_now, grad_act, gain_row):
    _, pullback = jax.vjp(lambda floats: activate(floats, gain_row), values.astype(jnp.float32))
    (through,) = pullback(grad_act)
    summed = grad_live.astype(jnp.float32) + through
    result = jnp.where(live_now[:, None], summed, jnp.zeros_like(summed))
    return result.astype(jnp.bfloat16)


def shards(segment_inputs, out_cotangent, neighbours, block_counts, norm_gain, kernel):
    n_pipe = lax.axis_size("pipe")
    n_x = lax.axis_size("sx")
    n_y = lax.axis_size("sy")
    segment_place = lax.axis_index("pipe")
    micro_count = segment_inputs.shape[1]
    row_count = segment_inputs.shape[4]
    channels = segment_inputs.shape[5]
    blocks = row_count // 512
    taps = 27
    gain_row = norm_gain[0]
    inputs = segment_inputs[0, :, 0, 0]
    cotangent = out_cotangent[:, 0, 0]
    tables = neighbours[:, 0, 0]
    slot_ids = jnp.arange(row_count, dtype=jnp.int32) // 512
    live_rows = slot_ids[None, :] < block_counts[:, 0, 0][:, None]

    def cube(values):
        return values.reshape(blocks, 8, 8, 8, channels)

    grads_out = []
    kernel_total = jnp.zeros((taps * channels, channels), jnp.float32)
    norm_scale = float(n_x * n_y * micro_count * row_count) ** (-0.5)
    shard_rows = kernel.shape[1]
    kernel_term = None
    for micro in range(micro_count):
        table = tables[micro]
        live_now = live_rows[micro]
        values = inputs[micro]
        activation = activate(values, gain_row).astype(jnp.bfloat16)
        start = cotangent[micro]
        start = jnp.where(live_now[:, None], start, jnp.zeros_like(start))
        both = jnp.concatenate([cube(activation), cube(start)], axis=-1)
        if micro == 0:
            carried = {}
            riding = kernel[0] if n_x >= 3 else None
            got = exchange(both, ("sx", "sy"), (n_x, n_y), 0, riding, carried)
            weights = gathered(kernel[0], "sx", carried)
            flipped = weights.reshape(3, 3, 3, channels, channels)[::-1, ::-1, ::-1].transpose(0, 1, 2, 4, 3)
        else:
            got = exchange(both, ("sx", "sy"), (n_x, n_y), 0)
        both_pad = assemble(both, got, table, split=True)
        act_pad = both_pad[..., :channels]
        centre = start
        received = None
        kept_dy = start
        kept_grad = jnp.zeros((row_count, channels), jnp.bfloat16)
        for tick in range(n_pipe):
            active = segment_place == n_pipe - 1 - tick
            kept_dy = jnp.where(active, centre, kept_dy)
            if tick == n_pipe - 1:
                per_tap = conv_filter(act_pad, cube(kept_dy))
                kernel_total = kernel_total + per_tap.transpose(1, 2, 3, 0, 4).reshape(taps * channels, channels)
                if micro == micro_count - 1:
                    kernel_term = (kernel_total * norm_scale).astype(jnp.bfloat16)
                    kernel_term, centre, received, both_pad = lax.optimization_barrier(
                        (kernel_term, centre, received, both_pad)
                    )
            grad_pad = both_pad[..., channels:] if tick == 0 else assemble(cube(centre), received, table)
            grad_act = conv_data(grad_pad, flipped).reshape(row_count, channels)
            result = finish_grad(values, centre, live_now, grad_act, gain_row)
            kept_grad = jnp.where(active, result, kept_grad)
            if tick < n_pipe - 1:
                down = [(p, p - 1) for p in range(1, n_pipe)]
                centre = lax.ppermute(result, "pipe", down)
                received = exchange(cube(result), ("pipe", "sx", "sy"), (n_pipe, n_x, n_y), 1)
        grads_out.append(kept_grad)
    grad_store = jnp.stack(grads_out)
    over_x = scattered_sum(kernel_term, "sx", shard_rows)
    partner = lax.ppermute(over_x, "sy", [(i, i ^ 1) for i in range(n_y)]) if n_y == 2 else None
    if partner is not None:
        kernel_share = over_x + partner
    else:
        kernel_share = lax.psum(over_x, "sy")
    return (grad_store[None, :, None, None], kernel_share[None])


def solution(mesh):
    return jax.shard_map(
        shards,
        mesh=mesh,
        in_specs=(
            P("pipe", None, "sx", "sy", None, None),
            P(None, "sx", "sy", None, None),
            P(None, "sx", "sy", None, None),
            P(None, "sx", "sy"),
            P("pipe", None),
            P("pipe", "sx", None),
        ),
        out_specs=(P("pipe", None, "sx", "sy", None, None), P("pipe", "sx", None)),
        check_vma=False,
    )
```

```python
import jax
import jax.numpy as jnp
from jax import lax
from jax.sharding import PartitionSpec as P

OFFSETS = (-1, 0, 1)


def source_range(offset):
    if offset < 0:
        return slice(7, 8)
    if offset > 0:
        return slice(0, 1)
    return slice(0, 8)


def activate(values, gain_row):
    floats = values.astype(jnp.float32)
    square = jnp.mean(floats * floats, axis=-1, keepdims=True)
    return jax.nn.silu(floats * lax.rsqrt(square + 1e-06) * gain_row)


def with_blank(blocks_in):
    return jnp.concatenate([blocks_in, jnp.zeros_like(blocks_in)], axis=0)


def face_piece(cube, shift_x, shift_y):
    return cube[:, source_range(shift_x), source_range(shift_y)]


def directions():
    return [(sx, sy) for sx in OFFSETS for sy in OFFSETS if (sx, sy) != (0, 0)]


def assemble(centre, received, table, split=False):
    slabs_x = []
    for shift_x in OFFSETS:
        rows_y = []
        for shift_y in OFFSETS:
            column = (shift_x + 1) * 3 + (shift_y + 1)
            piece = centre if (shift_x, shift_y) == (0, 0) else received[(shift_x, shift_y)]
            source = with_blank(piece)
            parts_z = []
            for shift_z in OFFSETS:
                direction = column * 3 + shift_z + 1
                if piece.shape[0] == 1:
                    chosen = table[:, direction][:, None, None, None, None] == 0
                    picked = jnp.where(chosen, piece, jnp.zeros_like(piece))
                else:
                    picked = source[table[:, direction]]
                parts_z.append(picked[:, :, :, source_range(shift_z), :])
            rows_y.append(jnp.concatenate(parts_z, axis=3))
        slabs_x.append(jnp.concatenate(rows_y, axis=2))
    if split:
        slabs_x[0], slabs_x[2] = lax.optimization_barrier((slabs_x[0], slabs_x[2]))
    return jnp.concatenate(slabs_x, axis=1)


def exchange(cube, axes, sizes, pipe_step, carry=None, carried=None):
    n_pipe, n_x, n_y = sizes if pipe_step else (pipe_step + 1, *sizes)

    def linear(p, a, b):
        return (p * n_x + a) * n_y + b if pipe_step else a * n_y + b

    def send(piece, moves):
        route = []
        for p in range(pipe_step, n_pipe):
            for a in range(n_x):
                for b in range(n_y):
                    ta, tb = moves(a, b)
                    if 0 <= ta < n_x and 0 <= tb < n_y:
                        route.append((linear(p, a, b), linear(p - pipe_step, ta, tb)))
        return lax.ppermute(piece, axes, route)

    def face_x(shift_x):
        face = face_piece(cube, shift_x, 0)
        if carry is None:
            return send(face, lambda a, b: (a - shift_x, b))
        rows = carry.shape[-1]
        payload = jnp.concatenate([carry, face.reshape(-1, rows)], axis=0)
        got = send(payload, lambda a, b: ((a - shift_x) % n_x, b))
        carried[(-shift_x) % n_x] = got[: carry.shape[0]]
        return got[carry.shape[0] :].reshape(face.shape)

    received = {}
    if n_y == 2:
        place_y = lax.axis_index("sy")
        for shift_x in OFFSETS:
            if shift_x != 0:
                received[(shift_x, 0)] = face_x(shift_x)
            row = lax.dynamic_slice_in_dim(cube[:, source_range(shift_x)], (1 - place_y) * 7, 1, axis=2)
            got = send(row, lambda a, b, i=shift_x: (a - i, 1 - b))
            received[(shift_x, 1)] = got
            received[(shift_x, -1)] = got
        return received
    for shift_x, shift_y in directions():
        if shift_y == 0:
            received[(shift_x, 0)] = face_x(shift_x)
            continue
        received[(shift_x, shift_y)] = send(
            face_piece(cube, shift_x, shift_y), lambda a, b, i=shift_x, j=shift_y: (a - i, b - j)
        )
    return received


def conv_data(padded, filters):
    return lax.conv_general_dilated(
        padded,
        filters,
        (1, 1, 1),
        "VALID",
        dimension_numbers=("NDHWC", "DHWIO", "NDHWC"),
        preferred_element_type=jnp.float32,
    )


def conv_filter(padded, grad_cube):
    return lax.conv_general_dilated(
        padded,
        grad_cube,
        (1, 1, 1),
        "VALID",
        dimension_numbers=("CDHWN", "IDHWO", "NDHWC"),
        preferred_element_type=jnp.float32,
    )


def gathered(shard, axis, given):
    count = lax.axis_size(axis)
    place = lax.axis_index(axis)
    parts = [shard]
    for step in range(1, count):
        if step in given:
            parts.append(given[step])
        else:
            parts.append(lax.ppermute(shard, axis, [(i, (i + step) % count) for i in range(count)]))
    backwards = jnp.stack(parts[::-1] * 2)
    ordered = lax.dynamic_slice_in_dim(backwards, count - 1 - place, count, axis=0)
    return ordered.reshape(count * shard.shape[0], *shard.shape[1:])


def scattered_sum(full, axis, share_rows):
    count = lax.axis_size(axis)
    place = lax.axis_index(axis)
    total = lax.dynamic_slice_in_dim(full, place * share_rows, share_rows, axis=0).astype(jnp.float32)
    for step in range(1, count):
        target = (place + step) % count
        piece = lax.dynamic_slice_in_dim(full, target * share_rows, share_rows, axis=0)
        total = total + lax.ppermute(piece, axis, [(i, (i + step) % count) for i in range(count)]).astype(
            jnp.float32
        )
    return total


def finish_grad(values, grad_live, live_now, grad_act, gain_row):
    _, pullback = jax.vjp(lambda floats: activate(floats, gain_row), values.astype(jnp.float32))
    (through,) = pullback(grad_act)
    summed = grad_live.astype(jnp.float32) + through
    result = jnp.where(live_now[:, None], summed, jnp.zeros_like(summed))
    return result.astype(jnp.bfloat16)


def shards(segment_inputs, out_cotangent, neighbours, block_counts, norm_gain, kernel):
    n_pipe = lax.axis_size("pipe")
    n_x = lax.axis_size("sx")
    n_y = lax.axis_size("sy")
    segment_place = lax.axis_index("pipe")
    micro_count = segment_inputs.shape[1]
    row_count = segment_inputs.shape[4]
    channels = segment_inputs.shape[5]
    blocks = row_count // 512
    taps = 27
    gain_row = norm_gain[0]
    inputs = segment_inputs[0, :, 0, 0]
    cotangent = out_cotangent[:, 0, 0]
    tables = neighbours[:, 0, 0]
    slot_ids = jnp.arange(row_count, dtype=jnp.int32) // 512
    live_rows = slot_ids[None, :] < block_counts[:, 0, 0][:, None]

    def cube(values):
        return values.reshape(blocks, 8, 8, 8, channels)

    grads_out = []
    kernel_total = jnp.zeros((taps * channels, channels), jnp.float32)
    norm_scale = float(n_x * n_y * micro_count * row_count) ** (-0.5)
    shard_rows = kernel.shape[1]
    kernel_term = None
    for micro in range(micro_count):
        table = tables[micro]
        live_now = live_rows[micro]
        values = inputs[micro]
        activation = activate(values, gain_row).astype(jnp.bfloat16)
        start = cotangent[micro]
        start = jnp.where(live_now[:, None], start, jnp.zeros_like(start))
        both = jnp.concatenate([cube(activation), cube(start)], axis=-1)
        if micro == 0:
            carried = {}
            riding = kernel[0] if n_x >= 3 else None
            got = exchange(both, ("sx", "sy"), (n_x, n_y), 0, riding, carried)
            weights = gathered(kernel[0], "sx", carried)
            flipped = weights.reshape(3, 3, 3, channels, channels)[::-1, ::-1, ::-1].transpose(0, 1, 2, 4, 3)
        else:
            got = exchange(both, ("sx", "sy"), (n_x, n_y), 0)
        both_pad = assemble(both, got, table, split=True)
        act_pad = both_pad[..., :channels]
        centre = start
        received = None
        kept_dy = start
        kept_grad = jnp.zeros((row_count, channels), jnp.bfloat16)
        for tick in range(n_pipe):
            active = segment_place == n_pipe - 1 - tick
            kept_dy = jnp.where(active, centre, kept_dy)
            if tick == n_pipe - 1:
                per_tap = conv_filter(act_pad, cube(kept_dy))
                kernel_total = kernel_total + per_tap.transpose(1, 2, 3, 0, 4).reshape(taps * channels, channels)
                if micro == micro_count - 1:
                    kernel_term = (kernel_total * norm_scale).astype(jnp.bfloat16)
                    kernel_term, centre, received, both_pad = lax.optimization_barrier(
                        (kernel_term, centre, received, both_pad)
                    )
            grad_pad = both_pad[..., channels:] if tick == 0 else assemble(cube(centre), received, table)
            grad_act = conv_data(grad_pad, flipped).reshape(row_count, channels)
            result = finish_grad(values, centre, live_now, grad_act, gain_row)
            kept_grad = jnp.where(active, result, kept_grad)
            if tick < n_pipe - 1:
                down = [(p, p - 1) for p in range(1, n_pipe)]
                centre = lax.ppermute(result, "pipe", down)
                received = exchange(cube(result), ("pipe", "sx", "sy"), (n_pipe, n_x, n_y), 1)
        grads_out.append(kept_grad)
    grad_store = jnp.stack(grads_out)
    over_x = scattered_sum(kernel_term, "sx", shard_rows)
    partner = lax.ppermute(over_x, "sy", [(i, i ^ 1) for i in range(n_y)]) if n_y == 2 else None
    if partner is not None:
        kernel_share = over_x + partner
    else:
        kernel_share = lax.psum(over_x, "sy")
    return (grad_store[None, :, None, None], kernel_share[None])


def solution(mesh):
    return jax.shard_map(
        shards,
        mesh=mesh,
        in_specs=(
            P("pipe", None, "sx", "sy", None, None),
            P(None, "sx", "sy", None, None),
            P(None, "sx", "sy", None, None),
            P(None, "sx", "sy"),
            P("pipe", None),
            P("pipe", "sx", None),
        ),
        out_specs=(P("pipe", None, "sx", "sy", None, None), P("pipe", "sx", None)),
        check_vma=False,
    )
```

```python
import jax
import jax.numpy as jnp
from jax import lax
from jax.sharding import PartitionSpec as P

OFFSETS = (-1, 0, 1)


def source_range(offset):
    if offset < 0:
        return slice(7, 8)
    if offset > 0:
        return slice(0, 1)
    return slice(0, 8)


def activate(values, gain_row):
    floats = values.astype(jnp.float32)
    square = jnp.mean(floats * floats, axis=-1, keepdims=True)
    return jax.nn.silu(floats * lax.rsqrt(square + 1e-06) * gain_row)


def with_blank(blocks_in):
    return jnp.concatenate([blocks_in, jnp.zeros_like(blocks_in)], axis=0)


def face_piece(cube, shift_x, shift_y):
    return cube[:, source_range(shift_x), source_range(shift_y)]


def directions():
    return [(sx, sy) for sx in OFFSETS for sy in OFFSETS if (sx, sy) != (0, 0)]


def assemble(centre, received, table, split=False):
    slabs_x = []
    for shift_x in OFFSETS:
        rows_y = []
        for shift_y in OFFSETS:
            column = (shift_x + 1) * 3 + (shift_y + 1)
            piece = centre if (shift_x, shift_y) == (0, 0) else received[(shift_x, shift_y)]
            source = with_blank(piece)
            parts_z = []
            for shift_z in OFFSETS:
                direction = column * 3 + shift_z + 1
                if piece.shape[0] == 1:
                    chosen = table[:, direction][:, None, None, None, None] == 0
                    picked = jnp.where(chosen, piece, jnp.zeros_like(piece))
                else:
                    picked = source[table[:, direction]]
                parts_z.append(picked[:, :, :, source_range(shift_z), :])
            rows_y.append(jnp.concatenate(parts_z, axis=3))
        slabs_x.append(jnp.concatenate(rows_y, axis=2))
    if split:
        slabs_x[0], slabs_x[2] = lax.optimization_barrier((slabs_x[0], slabs_x[2]))
    return jnp.concatenate(slabs_x, axis=1)


def exchange(cube, axes, sizes, pipe_step, carry=None, carried=None):
    n_pipe, n_x, n_y = sizes if pipe_step else (pipe_step + 1, *sizes)

    def linear(p, a, b):
        return (p * n_x + a) * n_y + b if pipe_step else a * n_y + b

    def send(piece, moves):
        route = []
        for p in range(pipe_step, n_pipe):
            for a in range(n_x):
                for b in range(n_y):
                    ta, tb = moves(a, b)
                    if 0 <= ta < n_x and 0 <= tb < n_y:
                        route.append((linear(p, a, b), linear(p - pipe_step, ta, tb)))
        return lax.ppermute(piece, axes, route)

    def face_x(shift_x):
        face = face_piece(cube, shift_x, 0)
        if carry is None:
            return send(face, lambda a, b: (a - shift_x, b))
        rows = carry.shape[-1]
        payload = jnp.concatenate([carry, face.reshape(-1, rows)], axis=0)
        got = send(payload, lambda a, b: ((a - shift_x) % n_x, b))
        carried[(-shift_x) % n_x] = got[: carry.shape[0]]
        return got[carry.shape[0] :].reshape(face.shape)

    received = {}
    if n_y == 2:
        place_y = lax.axis_index("sy")
        for shift_x in OFFSETS:
            if shift_x != 0:
                received[(shift_x, 0)] = face_x(shift_x)
            row = lax.dynamic_slice_in_dim(cube[:, source_range(shift_x)], (1 - place_y) * 7, 1, axis=2)
            got = send(row, lambda a, b, i=shift_x: (a - i, 1 - b))
            received[(shift_x, 1)] = got
            received[(shift_x, -1)] = got
        return received
    for shift_x, shift_y in directions():
        if shift_y == 0:
            received[(shift_x, 0)] = face_x(shift_x)
            continue
        received[(shift_x, shift_y)] = send(
            face_piece(cube, shift_x, shift_y), lambda a, b, i=shift_x, j=shift_y: (a - i, b - j)
        )
    return received


def conv_data(padded, filters):
    return lax.conv_general_dilated(
        padded,
        filters,
        (1, 1, 1),
        "VALID",
        dimension_numbers=("NDHWC", "DHWIO", "NDHWC"),
        preferred_element_type=jnp.float32,
    )


def conv_filter(padded, grad_cube):
    return lax.conv_general_dilated(
        padded,
        grad_cube,
        (1, 1, 1),
        "VALID",
        dimension_numbers=("CDHWN", "IDHWO", "NDHWC"),
        preferred_element_type=jnp.float32,
    )


def gathered(shard, axis, given):
    count = lax.axis_size(axis)
    place = lax.axis_index(axis)
    parts = [shard]
    for step in range(1, count):
        if step in given:
            parts.append(given[step])
        else:
            parts.append(lax.ppermute(shard, axis, [(i, (i + step) % count) for i in range(count)]))
    ordered = jnp.stack(parts)
    index = (place - jnp.arange(count)) % count
    slots = jnp.zeros((count,), jnp.int32).at[index].set(jnp.arange(count, dtype=jnp.int32))
    return ordered[slots].reshape(count * shard.shape[0], *shard.shape[1:])


def scattered_sum(full, axis, share_rows):
    count = lax.axis_size(axis)
    place = lax.axis_index(axis)
    total = lax.dynamic_slice_in_dim(full, place * share_rows, share_rows, axis=0).astype(jnp.float32)
    for step in range(1, count):
        target = (place + step) % count
        piece = lax.dynamic_slice_in_dim(full, target * share_rows, share_rows, axis=0)
        total = total + lax.ppermute(piece, axis, [(i, (i + step) % count) for i in range(count)]).astype(
            jnp.float32
        )
    return total


def finish_grad(values, grad_live, live_now, grad_act, gain_row):
    _, pullback = jax.vjp(lambda floats: activate(floats, gain_row), values.astype(jnp.float32))
    (through,) = pullback(grad_act)
    summed = grad_live.astype(jnp.float32) + through
    result = jnp.where(live_now[:, None], summed, jnp.zeros_like(summed))
    return result.astype(jnp.bfloat16)


def shards(segment_inputs, out_cotangent, neighbours, block_counts, norm_gain, kernel):
    n_pipe = lax.axis_size("pipe")
    n_x = lax.axis_size("sx")
    n_y = lax.axis_size("sy")
    segment_place = lax.axis_index("pipe")
    micro_count = segment_inputs.shape[1]
    row_count = segment_inputs.shape[4]
    channels = segment_inputs.shape[5]
    blocks = row_count // 512
    taps = 27
    gain_row = norm_gain[0]
    inputs = segment_inputs[0, :, 0, 0]
    cotangent = out_cotangent[:, 0, 0]
    tables = neighbours[:, 0, 0]
    slot_ids = jnp.arange(row_count, dtype=jnp.int32) // 512
    live_rows = slot_ids[None, :] < block_counts[:, 0, 0][:, None]

    def cube(values):
        return values.reshape(blocks, 8, 8, 8, channels)

    grads_out = []
    kernel_total = jnp.zeros((taps * channels, channels), jnp.float32)
    norm_scale = float(n_x * n_y * micro_count * row_count) ** (-0.5)
    shard_rows = kernel.shape[1]
    kernel_term = None
    for micro in range(micro_count):
        table = tables[micro]
        live_now = live_rows[micro]
        values = inputs[micro]
        activation = activate(values, gain_row).astype(jnp.bfloat16)
        start = cotangent[micro]
        start = jnp.where(live_now[:, None], start, jnp.zeros_like(start))
        both = jnp.concatenate([cube(activation), cube(cotangent[micro])], axis=-1)
        own = jnp.concatenate([cube(activation), cube(start)], axis=-1)
        if micro == 0:
            carried = {}
            riding = kernel[0] if n_x >= 3 else None
            got = exchange(both, ("sx", "sy"), (n_x, n_y), 0, riding, carried)
            weights = gathered(kernel[0], "sx", carried)
            flipped = weights.reshape(3, 3, 3, channels, channels)[::-1, ::-1, ::-1].transpose(0, 1, 2, 4, 3)
        else:
            got = exchange(both, ("sx", "sy"), (n_x, n_y), 0)
        both_pad = assemble(own, got, table, split=True)
        act_pad = both_pad[..., :channels]
        centre = start
        received = None
        kept_dy = start
        kept_grad = jnp.zeros((row_count, channels), jnp.bfloat16)
        for tick in range(n_pipe):
            active = segment_place == n_pipe - 1 - tick
            kept_dy = jnp.where(active, centre, kept_dy)
            if tick == n_pipe - 1:
                per_tap = conv_filter(act_pad, cube(kept_dy))
                kernel_total = kernel_total + per_tap.transpose(1, 2, 3, 0, 4).reshape(taps * channels, channels)
                if micro == micro_count - 1:
                    kernel_term = (kernel_total * norm_scale).astype(jnp.bfloat16)
                    kernel_term, centre, received, both_pad = lax.optimization_barrier(
                        (kernel_term, centre, received, both_pad)
                    )
            grad_pad = both_pad[..., channels:] if tick == 0 else assemble(cube(centre), received, table)
            grad_act = conv_data(grad_pad, flipped).reshape(row_count, channels)
            result = finish_grad(values, centre, live_now, grad_act, gain_row)
            kept_grad = jnp.where(active, result, kept_grad)
            if tick < n_pipe - 1:
                down = [(p, p - 1) for p in range(1, n_pipe)]
                centre = lax.ppermute(result, "pipe", down)
                received = exchange(cube(result), ("pipe", "sx", "sy"), (n_pipe, n_x, n_y), 1)
        grads_out.append(kept_grad)
    grad_store = jnp.stack(grads_out)
    over_x = scattered_sum(kernel_term, "sx", shard_rows)
    partner = lax.ppermute(over_x, "sy", [(i, i ^ 1) for i in range(n_y)]) if n_y == 2 else None
    if partner is not None:
        kernel_share = over_x + partner
    else:
        kernel_share = lax.psum(over_x, "sy")
    return (grad_store[None, :, None, None], kernel_share[None])


def solution(mesh):
    return jax.shard_map(
        shards,
        mesh=mesh,
        in_specs=(
            P("pipe", None, "sx", "sy", None, None),
            P(None, "sx", "sy", None, None),
            P(None, "sx", "sy", None, None),
            P(None, "sx", "sy"),
            P("pipe", None),
            P("pipe", "sx", None),
        ),
        out_specs=(P("pipe", None, "sx", "sy", None, None), P("pipe", "sx", None)),
        check_vma=False,
    )
```
